128 devices in a mesh: sector: 8 (over y, core), row: 16 (over x, z).
Axes of the slice: x: 4, y: 4, z: 4, core: 2. Of those that a mesh axis runs over, the one named last changes fastest.
Arguments:
- amplitudes: bfloat16 [8192, 4, 8192], P('sector', None, 'row'), may hold values from -6 to 6
- next_site: bfloat16 [8, 4, 8192, 2048], P('sector', None, 'row'), may hold values from -0.03125 to 0.03125
- sector_rows: int32 [8], replicated, may hold values from 512 to 1024, as said below
- moves: int32 [2, 8], replicated, may hold values from 0 to 128, as said below
- angles: float32 [2, 8, 128], replicated, may hold values from -3.140625 to 3.140625
- ranks: int32 [8], replicated, may hold values from 256 to 1024, as said below
Outputs:
- canonical: bfloat16 [2048, 8192], P('row', 'sector')
The draws below stay inside these ranges and needn't reach their ends.
Inputs may be any that keep to these rules, and one draw needn't show every extreme that they name: `sector_rows`: one sector has exactly 1024 live rows and another exactly 512. `moves`: the entry of the last sector is 0, every other entry is 1 or more; for each gate some pair moves exactly 128 rows. `ranks`: each sector keeps at least half of its live rows and at most all of them; one sector keeps 1024 rows and one keeps 1024 // 4.
All inputs are finite; a program needn't handle non-finite values.
Results may differ from the reference program's by a relative error of at most 0.014.
Values may be sent and summed in bfloat16 or wider, within the bound.
No kernel may reach another device: no remote copies, remote signals or barrier semaphores. Data moves between devices by JAX's collectives and lax.ppermute only.
A program may use at most 128 MiB of HBM per device.

```python
import math
import jax
import jax.numpy as jnp
from jax import lax

LSEC = 1024
PHYS = 4
RB = 8192
KOUT = 2048
MOVE = 128
SECTORS = 8


def sector_plan(key):
    keys = jax.random.split(jax.random.fold_in(key, 7), 5)
    sector_index = jnp.arange(SECTORS)
    center = SECTORS // 2
    live_rows = jax.random.randint(keys[0], (SECTORS,), LSEC // 2, LSEC + 1)
    smallest = jax.random.randint(keys[1], (), 0, SECTORS - 1)
    smallest = jnp.where(smallest >= center, smallest + 1, smallest)
    live_rows = jnp.where(sector_index == center, LSEC, live_rows)
    live_rows = jnp.where(sector_index == smallest, LSEC // 2, live_rows)
    spread = jax.random.randint(keys[2], (SECTORS,), 0, 1 << 20)
    kept_rows = live_rows // 2 + spread % (live_rows - live_rows // 2 + 1)
    kept_rows = jnp.where(sector_index == center, LSEC, kept_rows)
    kept_rows = jnp.where(sector_index == smallest, LSEC // 4, kept_rows)
    pair_rows = jax.random.randint(keys[3], (2, SECTORS), 1, MOVE + 1)
    fullest = jax.random.randint(keys[4], (2,), 0, SECTORS - 1)
    pair_rows = jnp.where(sector_index[None, :] == fullest[:, None], MOVE, pair_rows)
    pair_rows = jnp.where(sector_index[None, :] == SECTORS - 1, 0, pair_rows)
    return (live_rows.astype(jnp.int32), pair_rows.astype(jnp.int32), kept_rows.astype(jnp.int32))


def draw_sector_rows(key, part):
    return sector_plan(key)[0]


def draw_moves(key, part):
    return sector_plan(key)[1]


def draw_ranks(key, part):
    return sector_plan(key)[2]


def block_levels(rng, dims, shards, low, largest):
    def one(dim, parts):
        steps = jax.random.uniform(jax.random.fold_in(jax.random.fold_in(rng, 6), dim), (parts,), jnp.float32, low / len(shards), largest / len(shards))
        return jnp.repeat(jnp.exp(steps), dims[dim] // parts).reshape((-1,) + (1,) * (len(dims) - dim - 1))

    gain = one(*shards[0])
    for cut in shards[1:]:
        gain = gain * one(*cut)
    return gain


def bell_draw(own_key, dims, deviation, reach, cuts=(), held_as=jnp.bfloat16):
    array = jax.random.normal(own_key, dims, jnp.float32) * deviation
    if len(cuts) > 0:
        array = block_levels(own_key, dims, cuts, -0.22, 0.18) * array
    return jnp.clip(array, min=-reach, max=reach).astype(held_as)


def setup_inputs(seed: int = 0) -> dict:
    splits = jax.random.split(jax.random.key(seed), 7)
    amplitudes = bell_draw(splits[0], (SECTORS * LSEC, PHYS, RB), 1.0, 6.0, ((0, 8), (2, 16)))
    next_site = bell_draw(splits[1], (SECTORS, PHYS, RB, KOUT), (PHYS * RB) ** -0.5, 0.03125, ((0, 8), (2, 16)))
    sector_rows = draw_sector_rows(jax.random.fold_in(splits[6], 71), 0)
    moves = draw_moves(jax.random.fold_in(splits[6], 71), 0)
    angles = jnp.clip(jax.random.uniform(splits[4], (2, SECTORS, MOVE), jnp.float32, -3.140625, 3.140625), -3.140625, 3.140625)
    ranks = draw_ranks(jax.random.fold_in(splits[6], 71), 0)
    return {"amplitudes": amplitudes, "next_site": next_site, "sector_rows": sector_rows, "moves": moves, "angles": angles, "ranks": ranks}


def reference(amplitudes, next_site, sector_rows, moves, angles, ranks):
    blocks = amplitudes.astype(jnp.float32).reshape(SECTORS, LSEC, PHYS, RB)
    row_index = jnp.arange(LSEC)
    padded = []
    for sector in range(SECTORS):
        live_rows = jnp.where((row_index < sector_rows[sector])[:, None, None], blocks[sector], jnp.float32(0.0))
        padded.append(jnp.concatenate([live_rows, jnp.zeros((MOVE, PHYS, RB), jnp.float32)], 0))
    slot_index = jnp.arange(MOVE)
    for gate_index in range(2):
        for sector in range(SECTORS - 1):
            pair_count = moves[gate_index, sector]
            if gate_index == 0:
                start_a = (sector_rows[sector] - moves[0, sector]).astype(jnp.int32)
                start_b = jnp.int32(0)
            else:
                start_a = (sector_rows[sector] - moves[0, sector] - moves[1, sector]).astype(jnp.int32)
                start_b = moves[0, sector].astype(jnp.int32)
            rows_a = lax.dynamic_slice_in_dim(padded[sector], start_a, MOVE, 0)
            rows_b = lax.dynamic_slice_in_dim(padded[sector + 1], start_b, MOVE, 0)
            angle_row = angles[gate_index, sector][:, None, None]
            valid = (slot_index < pair_count)[:, None, None]
            new_a = jnp.where(valid, jnp.cos(angle_row) * rows_a - jnp.sin(angle_row) * rows_b, rows_a)
            new_b = jnp.where(valid, jnp.sin(angle_row) * rows_a + jnp.cos(angle_row) * rows_b, rows_b)
            padded[sector] = lax.dynamic_update_slice_in_dim(padded[sector], new_a, start_a, 0)
            padded[sector + 1] = lax.dynamic_update_slice_in_dim(padded[sector + 1], new_b, start_b, 0)
    results = []
    for sector in range(SECTORS):
        block_rows = padded[sector][:LSEC].astype(jnp.bfloat16)
        contracted = jnp.einsum('prk,lpr->kl', next_site[sector].astype(jnp.float32), block_rows.astype(jnp.float32), precision=lax.Precision.HIGHEST).astype(jnp.bfloat16)
        wide_rows = contracted.astype(jnp.float32)
        dead_rows = (row_index >= sector_rows[sector]).astype(jnp.float32)
        gram_matrix = jnp.dot(wide_rows.T, wide_rows, precision=lax.Precision.HIGHEST) + jnp.diag(dead_rows)
        factor_low = jnp.linalg.cholesky(gram_matrix)
        solved = jax.scipy.linalg.solve_triangular(factor_low, wide_rows.T, lower=True).T
        kept_mask = ((row_index >= sector_rows[sector] - ranks[sector]) & (row_index < sector_rows[sector])).astype(jnp.float32)
        results.append((solved * math.sqrt(KOUT) * kept_mask[None, :]).astype(jnp.bfloat16))
    return jnp.concatenate(results, 1)
```

```python
import math

import jax
import jax.numpy as jnp
from jax import lax
from jax.sharding import PartitionSpec as P

KOUT = 2048
BLOCK = 128
HI = lax.Precision.HIGHEST


def shifted(x, axis, by):
    size = lax.axis_size(axis)
    pairs = [(i, i + by) for i in range(size) if 0 <= i + by < size]
    return lax.ppermute(x, axis, pairs)


def rotated_window(own, partner, angle, count, sign):
    slot_index = jnp.arange(own.shape[0])
    own32 = own.astype(jnp.float32)
    partner32 = partner.astype(jnp.float32)
    cos_t = jnp.cos(angle)[:, None, None]
    sin_t = jnp.sin(angle)[:, None, None]
    if sign < 0:
        new = cos_t * own32 - sin_t * partner32
    else:
        new = sin_t * partner32 + cos_t * own32
    return jnp.where((slot_index < count)[:, None, None], new, own32).astype(jnp.bfloat16)


def dot(a, b):
    return jnp.dot(a, b, precision=HI, preferred_element_type=jnp.float32)


def cholesky_solve(gram, rhs):
    n = gram.shape[0]
    eye = jnp.eye(BLOCK, dtype=jnp.float32)
    trailing = gram
    rest = rhs
    solved = []
    for start in range(0, n, BLOCK):
        diag = trailing[:BLOCK, :BLOCK]
        factor = jnp.linalg.cholesky(diag)
        inverse = lax.linalg.triangular_solve(factor, eye, left_side=True, lower=True)
        head = dot(inverse, rest[:BLOCK])
        solved.append(head)
        if start + BLOCK < n:
            panel = lax.dot_general(
                trailing[BLOCK:, :BLOCK], inverse, (((1,), (1,)), ((), ())),
                precision=HI, preferred_element_type=jnp.float32,
            )
            trailing = trailing[BLOCK:, BLOCK:] - lax.dot_general(
                panel, panel, (((1,), (1,)), ((), ())),
                precision=HI, preferred_element_type=jnp.float32,
            )
            rest = rest[BLOCK:] - dot(panel, head)
    return jnp.concatenate(solved, 0)


def per_device(amplitudes, next_site, sector_rows, moves, angles, ranks):
    sector_id = lax.axis_index("sector")
    rows = amplitudes.shape[0]
    move_rows = angles.shape[-1]
    row_index = jnp.arange(rows)
    live_rows = sector_rows[sector_id]
    prev_id = jnp.maximum(sector_id - 1, 0)
    count_here = moves[:, sector_id]
    count_prev = jnp.where(sector_id > 0, moves[:, prev_id], 0)
    masked = jnp.where((row_index < live_rows)[:, None, None], amplitudes, jnp.zeros((), amplitudes.dtype))
    padded = jnp.concatenate(
        [masked, jnp.zeros((move_rows,) + masked.shape[1:], masked.dtype)], 0
    )
    starts_a = [live_rows - count_here[0], live_rows - count_here[0] - count_here[1]]
    starts_b = [jnp.int32(0), count_prev[0]]
    own_a = [lax.dynamic_slice_in_dim(padded, s, move_rows, 0) for s in starts_a]
    own_b = [lax.dynamic_slice_in_dim(padded, s, move_rows, 0) for s in starts_b]
    from_below = [shifted(w, "sector", 1) for w in own_a]
    from_above = [shifted(w, "sector", -1) for w in own_b]
    new_a = [
        rotated_window(own_a[g], from_above[g], angles[g][sector_id], count_here[g], -1)
        for g in range(2)
    ]
    new_b = [
        rotated_window(own_b[g], from_below[g], angles[g][prev_id], count_prev[g], 1)
        for g in range(2)
    ]
    padded = lax.dynamic_update_slice_in_dim(padded, new_a[1], starts_a[1], 0)
    padded = lax.dynamic_update_slice_in_dim(padded, new_a[0], starts_a[0], 0)
    padded = lax.dynamic_update_slice_in_dim(padded, new_b[0], starts_b[0], 0)
    padded = lax.dynamic_update_slice_in_dim(padded, new_b[1], starts_b[1], 0)
    block_rows = padded[:rows]
    site_tensor = next_site[0]
    contracted = lax.psum_scatter(
        jnp.einsum("prk,lpr->kl", site_tensor, block_rows, preferred_element_type=jnp.float32),
        "row",
        scatter_dimension=0,
        tiled=True,
    ).astype(jnp.bfloat16)
    gathered = lax.all_gather(contracted, "row", axis=0, tiled=True)
    gram_matrix = lax.dot_general(
        gathered, gathered, (((0,), (0,)), ((), ())), preferred_element_type=jnp.float32
    )
    dead_rows = (row_index >= live_rows).astype(jnp.float32)
    gram_matrix = gram_matrix + jnp.diag(dead_rows)
    solved = cholesky_solve(gram_matrix, contracted.astype(jnp.float32).T).T
    kept_mask = ((row_index >= live_rows - ranks[sector_id]) & (row_index < live_rows)).astype(
        jnp.float32
    )
    return (solved * math.sqrt(KOUT) * kept_mask[None, :]).astype(jnp.bfloat16)


def solution(mesh):
    placed = (P("sector", None, "row"), P("sector", None, "row", None), P(), P(), P(), P())
    return jax.shard_map(
        per_device, mesh=mesh, in_specs=placed, out_specs=P("row", "sector"), check_vma=False
    )
```

```python
import math

import jax
import jax.numpy as jnp
from jax import lax
from jax.experimental import pallas as pl
from jax.sharding import PartitionSpec as P

KOUT = 2048
BLOCK = 128
HI = lax.Precision.HIGHEST


def shifted(x, axis, by):
    size = lax.axis_size(axis)
    pairs = [(i, i + by) for i in range(size) if 0 <= i + by < size]
    return lax.ppermute(x, axis, pairs)


def rotated_window(own, partner, angle, count, sign):
    slot_index = jnp.arange(own.shape[0])
    own32 = own.astype(jnp.float32)
    partner32 = partner.astype(jnp.float32)
    cos_t = jnp.cos(angle)[:, None, None]
    sin_t = jnp.sin(angle)[:, None, None]
    if sign < 0:
        new = cos_t * own32 - sin_t * partner32
    else:
        new = sin_t * partner32 + cos_t * own32
    return jnp.where((slot_index < count)[:, None, None], new, own32).astype(jnp.bfloat16)


def dot(a, b):
    return jnp.dot(a, b, precision=HI, preferred_element_type=jnp.float32)


def factor_inverse_kernel(d_ref, o_ref):
    n = d_ref.shape[0]
    lane = lax.broadcasted_iota(jnp.int32, (n, n), 1)
    sub = lax.broadcasted_iota(jnp.int32, (n, n), 0)
    lane_row = lax.broadcasted_iota(jnp.int32, (1, n), 1)
    sub_col = lax.broadcasted_iota(jnp.int32, (n, 1), 0)

    def body(j, carry):
        a, w = carry
        col = jnp.sum(jnp.where(lane == j, a, 0.0), axis=1, keepdims=True)
        row = jnp.sum(jnp.where(sub == j, a, 0.0), axis=0, keepdims=True)
        piv = jnp.sum(jnp.where(lane_row == j, row, 0.0), axis=1, keepdims=True)
        r = lax.rsqrt(piv)
        lcol = jnp.where(sub_col >= j, col * r, 0.0)
        lrow = jnp.where(lane_row >= j, row * r, 0.0)
        a = a - lcol * lrow
        wj = jnp.sum(jnp.where(sub == j, w, 0.0), axis=0, keepdims=True) * r
        w = jnp.where(sub == j, wj, w - lcol * wj)
        return a, w

    w0 = (sub == lane).astype(jnp.float32)
    _, w = lax.fori_loop(0, n, body, (d_ref[...], w0))
    o_ref[...] = w


def factor_inverse(diag):
    n = diag.shape[0]
    return pl.pallas_call(
        factor_inverse_kernel,
        out_shape=jax.ShapeDtypeStruct((n, n), jnp.float32),
        cost_estimate=pl.CostEstimate(
            flops=6 * n * n * n, transcendentals=n, bytes_accessed=8 * n * n
        ),
    )(diag)


def cholesky_solve(gram, rhs):
    n = gram.shape[0]
    trailing = gram
    rest = rhs
    solved = []
    for start in range(0, n, BLOCK):
        diag = trailing[:BLOCK, :BLOCK]
        inverse = factor_inverse(diag)
        head = dot(inverse, rest[:BLOCK])
        solved.append(head)
        if start + BLOCK < n:
            panel = lax.dot_general(
                trailing[BLOCK:, :BLOCK], inverse, (((1,), (1,)), ((), ())),
                precision=HI, preferred_element_type=jnp.float32,
            )
            trailing = trailing[BLOCK:, BLOCK:] - lax.dot_general(
                panel, panel, (((1,), (1,)), ((), ())),
                precision=HI, preferred_element_type=jnp.float32,
            )
            rest = rest[BLOCK:] - dot(panel, head)
    return jnp.concatenate(solved, 0)


def per_device(amplitudes, next_site, sector_rows, moves, angles, ranks):
    sector_id = lax.axis_index("sector")
    rows = amplitudes.shape[0]
    move_rows = angles.shape[-1]
    row_index = jnp.arange(rows)
    live_rows = sector_rows[sector_id]
    prev_id = jnp.maximum(sector_id - 1, 0)
    count_here = moves[:, sector_id]
    count_prev = jnp.where(sector_id > 0, moves[:, prev_id], 0)
    masked = jnp.where((row_index < live_rows)[:, None, None], amplitudes, jnp.zeros((), amplitudes.dtype))
    padded = jnp.concatenate(
        [masked, jnp.zeros((move_rows,) + masked.shape[1:], masked.dtype)], 0
    )
    starts_a = [live_rows - count_here[0], live_rows - count_here[0] - count_here[1]]
    starts_b = [jnp.int32(0), count_prev[0]]
    own_a = [lax.dynamic_slice_in_dim(padded, s, move_rows, 0) for s in starts_a]
    own_b = [lax.dynamic_slice_in_dim(padded, s, move_rows, 0) for s in starts_b]
    from_below = [shifted(w, "sector", 1) for w in own_a]
    from_above = [shifted(w, "sector", -1) for w in own_b]
    new_a = [
        rotated_window(own_a[g], from_above[g], angles[g][sector_id], count_here[g], -1)
        for g in range(2)
    ]
    new_b = [
        rotated_window(own_b[g], from_below[g], angles[g][prev_id], count_prev[g], 1)
        for g in range(2)
    ]
    padded = lax.dynamic_update_slice_in_dim(padded, new_a[1], starts_a[1], 0)
    padded = lax.dynamic_update_slice_in_dim(padded, new_a[0], starts_a[0], 0)
    padded = lax.dynamic_update_slice_in_dim(padded, new_b[0], starts_b[0], 0)
    padded = lax.dynamic_update_slice_in_dim(padded, new_b[1], starts_b[1], 0)
    block_rows = padded[:rows]
    site_tensor = next_site[0]
    contracted = lax.psum_scatter(
        jnp.einsum("prk,lpr->kl", site_tensor, block_rows, preferred_element_type=jnp.float32),
        "row",
        scatter_dimension=0,
        tiled=True,
    ).astype(jnp.bfloat16)
    gathered = lax.all_gather(contracted, "row", axis=0, tiled=True)
    gram_matrix = lax.dot_general(
        gathered, gathered, (((0,), (0,)), ((), ())), preferred_element_type=jnp.float32
    )
    dead_rows = (row_index >= live_rows).astype(jnp.float32)
    gram_matrix = gram_matrix + jnp.diag(dead_rows)
    solved = cholesky_solve(gram_matrix, contracted.astype(jnp.float32).T).T
    kept_mask = ((row_index >= live_rows - ranks[sector_id]) & (row_index < live_rows)).astype(
        jnp.float32
    )
    return (solved * math.sqrt(KOUT) * kept_mask[None, :]).astype(jnp.bfloat16)


def solution(mesh):
    placed = (P("sector", None, "row"), P("sector", None, "row", None), P(), P(), P(), P())
    return jax.shard_map(
        per_device, mesh=mesh, in_specs=placed, out_specs=P("row", "sector"), check_vma=False
    )
```

```python
import math

import jax
import jax.numpy as jnp
from jax import lax
from jax.experimental import pallas as pl
from jax.sharding import PartitionSpec as P

KOUT = 2048
BLOCK = 128
PHASE = 8
HI = lax.Precision.HIGHEST


def shifted(x, axis, by):
    size = lax.axis_size(axis)
    pairs = [(i, i + by) for i in range(size) if 0 <= i + by < size]
    return lax.ppermute(x, axis, pairs)


def frame_start(live, rows, span):
    return jnp.minimum((live - 2 * span) // 16 * 16, rows - 2 * span - 16)

def shift_rows(buf, by, length):
    lead = length
    ext = jnp.concatenate([jnp.zeros((lead,) + buf.shape[1:], buf.dtype), buf,
                           jnp.zeros((length,) + buf.shape[1:], buf.dtype)], 0)
    return lax.dynamic_slice_in_dim(ext, lead + by, length, 0)

def take_angles(vec, idx, valid):
    return jnp.where(valid, jnp.take(vec, jnp.clip(idx, 0, vec.shape[0] - 1)), 0.0)

def build_block(amplitudes, sector_rows, moves, angles):
    sector_id = lax.axis_index("sector")
    nsec = lax.axis_size("sector")
    rows = amplitudes.shape[0]
    span = angles.shape[-1]
    live = sector_rows[sector_id]
    prev_id = jnp.maximum(sector_id - 1, 0)
    live_prev = sector_rows[prev_id]
    m0h, m1h = moves[0, sector_id], moves[1, sector_id]
    m0p = jnp.where(sector_id > 0, moves[0, prev_id], 0)
    m1p = jnp.where(sector_id > 0, moves[1, prev_id], 0)
    row_index = jnp.arange(rows)
    masked = jnp.where((row_index < live)[:, None, None], amplitudes, jnp.zeros((), amplitudes.dtype))
    a_len = 2 * span + 16
    b_len = 2 * span
    fa = frame_start(live, rows, span)
    fa_prev = frame_start(live_prev, rows, span)
    a_frame = lax.dynamic_slice_in_dim(masked, fa, a_len, 0)
    b_frame = masked[:b_len]
    from_below = shifted(a_frame, "sector", 1)
    from_above = shifted(b_frame, "sector", -1)
    j = jnp.arange(a_len)
    i0 = j + fa - live + m0h
    i1 = j + fa - live + m0h + m1h
    v0 = (i0 >= 0) & (i0 < m0h)
    v1 = (i1 >= 0) & (i1 < m1h)
    p0 = shift_rows(from_above, fa - live + m0h, a_len)
    p1 = shift_rows(from_above, fa - live + 2 * m0h + m1h, a_len)
    ang = take_angles(angles[0][sector_id], i0, v0) + take_angles(angles[1][sector_id], i1, v1)
    partner = jnp.where(v0[:, None, None], p0, p1).astype(jnp.float32)
    own = a_frame.astype(jnp.float32)
    c = jnp.cos(ang)[:, None, None]
    s = jnp.sin(ang)[:, None, None]
    new_a = jnp.where((v0 | v1)[:, None, None], c * own - s * partner, own).astype(jnp.bfloat16)
    jb = jnp.arange(b_len)
    k0 = jb
    k1 = jb - m0p
    w0 = k0 < m0p
    w1 = (k1 >= 0) & (k1 < m1p)
    q0 = shift_rows(from_below, live_prev - m0p - fa_prev, b_len)
    q1 = shift_rows(from_below, live_prev - 2 * m0p - m1p - fa_prev, b_len)
    angb = take_angles(angles[0][prev_id], k0, w0) + take_angles(angles[1][prev_id], k1, w1)
    partner_b = jnp.where(w0[:, None, None], q0, q1).astype(jnp.float32)
    ownb = b_frame.astype(jnp.float32)
    cb = jnp.cos(angb)[:, None, None]
    sb = jnp.sin(angb)[:, None, None]
    new_b = jnp.where((w0 | w1)[:, None, None], sb * partner_b + cb * ownb, ownb).astype(jnp.bfloat16)
    block = lax.dynamic_update_slice_in_dim(masked, new_a, fa, 0)
    return lax.dynamic_update_slice_in_dim(block, new_b, 0, 0)


def dot(a, b):
    return jnp.dot(a, b, precision=HI, preferred_element_type=jnp.float32)


def factor_inverse_kernel(d_ref, o_ref):
    n = d_ref.shape[0]
    a = d_ref[...]
    eye_rows = lax.broadcasted_iota(jnp.int32, (n, n), 0)
    w = (eye_rows == lax.broadcasted_iota(jnp.int32, (n, n), 1)).astype(jnp.float32)
    for first in range(0, n, PHASE):
        m = n - first
        lane = lax.broadcasted_iota(jnp.int32, (m, n), 1)
        sub = lax.broadcasted_iota(jnp.int32, (m, n), 0)
        lane_row = lax.broadcasted_iota(jnp.int32, (1, n), 1)
        sub_col = lax.broadcasted_iota(jnp.int32, (m, 1), 0)

        def body(t, carry, first=first, lane=lane, sub=sub, lane_row=lane_row, sub_col=sub_col):
            a, w = carry
            j = first + t
            col = jnp.sum(jnp.where(lane == j, a, 0.0), axis=1, keepdims=True)
            row = jnp.sum(jnp.where(sub == t, a, 0.0), axis=0, keepdims=True)
            piv = jnp.sum(jnp.where(lane_row == j, row, 0.0), axis=1, keepdims=True)
            r = lax.rsqrt(piv)
            lcol = jnp.where(sub_col >= t, col * r, 0.0)
            lrow = jnp.where(lane_row >= j, row * r, 0.0)
            a = a - lcol * lrow
            wj = jnp.sum(jnp.where(sub == t, w, 0.0), axis=0, keepdims=True) * r
            w = jnp.where(sub == t, wj, w - lcol * wj)
            return a, w

        a, w = lax.fori_loop(0, PHASE, body, (a, w), unroll=PHASE)
        o_ref[first:first + PHASE, :] = w[:PHASE]
        a = a[PHASE:]
        w = w[PHASE:]


def factor_inverse(diag):
    n = diag.shape[0]
    return pl.pallas_call(
        factor_inverse_kernel,
        out_shape=jax.ShapeDtypeStruct((n, n), jnp.float32),
        cost_estimate=pl.CostEstimate(
            flops=6 * n * n * n, transcendentals=n, bytes_accessed=8 * n * n
        ),
    )(diag)


def cholesky_solve(gram, rhs):
    n = gram.shape[0]
    trailing = gram
    rest = rhs
    solved = []
    for start in range(0, n, BLOCK):
        diag = trailing[:BLOCK, :BLOCK]
        inverse = factor_inverse(diag)
        head = dot(inverse, rest[:BLOCK])
        solved.append(head)
        if start + BLOCK < n:
            panel = lax.dot_general(
                trailing[BLOCK:, :BLOCK], inverse, (((1,), (1,)), ((), ())),
                precision=HI, preferred_element_type=jnp.float32,
            )
            trailing = trailing[BLOCK:, BLOCK:] - lax.dot_general(
                panel, panel, (((1,), (1,)), ((), ())),
                precision=HI, preferred_element_type=jnp.float32,
            )
            rest = rest[BLOCK:] - dot(panel, head)
    return jnp.concatenate(solved, 0)


def per_device(amplitudes, next_site, sector_rows, moves, angles, ranks):
    sector_id = lax.axis_index("sector")
    rows = amplitudes.shape[0]
    row_index = jnp.arange(rows)
    live_rows = sector_rows[sector_id]
    block_rows = build_block(amplitudes, sector_rows, moves, angles)
    site_tensor = next_site[0]
    contracted = lax.psum_scatter(
        jnp.einsum("prk,lpr->kl", site_tensor, block_rows, preferred_element_type=jnp.float32),
        "row",
        scatter_dimension=0,
        tiled=True,
    ).astype(jnp.bfloat16)
    gathered = lax.all_gather(contracted, "row", axis=0, tiled=True)
    gram_matrix = lax.dot_general(
        gathered, gathered, (((0,), (0,)), ((), ())), preferred_element_type=jnp.float32
    )
    dead_rows = (row_index >= live_rows).astype(jnp.float32)
    gram_matrix = gram_matrix + jnp.diag(dead_rows)
    solved = cholesky_solve(gram_matrix, contracted.astype(jnp.float32).T).T
    kept_mask = ((row_index >= live_rows - ranks[sector_id]) & (row_index < live_rows)).astype(
        jnp.float32
    )
    return (solved * math.sqrt(KOUT) * kept_mask[None, :]).astype(jnp.bfloat16)


def solution(mesh):
    placed = (P("sector", None, "row"), P("sector", None, "row", None), P(), P(), P(), P())
    return jax.shard_map(
        per_device, mesh=mesh, in_specs=placed, out_specs=P("row", "sector"), check_vma=False
    )
```

```python
import math

import jax
import jax.numpy as jnp
from jax import lax
from jax.experimental import pallas as pl
from jax.sharding import PartitionSpec as P

KOUT = 2048
BLOCK = 128
PHASE = 8
HI = lax.Precision.HIGHEST


def shifted(x, axis, by):
    size = lax.axis_size(axis)
    pairs = [(i, i + by) for i in range(size) if 0 <= i + by < size]
    return lax.ppermute(x, axis, pairs)


def frame_start(live, rows, span):
    return jnp.minimum((live - 2 * span) // 16 * 16, rows - 2 * span - 16)

def shift_rows(buf, by, length):
    index = jnp.clip(jnp.arange(length) + by, 0, buf.shape[0] - 1)
    return jnp.take(buf, index, axis=0)


def take_angles(vec, idx, valid):
    return jnp.where(valid, jnp.take(vec, jnp.clip(idx, 0, vec.shape[0] - 1)), 0.0)

def build_block(amplitudes, sector_rows, moves, angles):
    sector_id = lax.axis_index("sector")
    nsec = lax.axis_size("sector")
    rows = amplitudes.shape[0]
    span = angles.shape[-1]
    live = sector_rows[sector_id]
    prev_id = jnp.maximum(sector_id - 1, 0)
    live_prev = sector_rows[prev_id]
    m0h, m1h = moves[0, sector_id], moves[1, sector_id]
    m0p = jnp.where(sector_id > 0, moves[0, prev_id], 0)
    m1p = jnp.where(sector_id > 0, moves[1, prev_id], 0)
    row_index = jnp.arange(rows)
    masked = jnp.where((row_index < live)[:, None, None], amplitudes, jnp.zeros((), amplitudes.dtype))
    a_len = 2 * span + 16
    b_len = 2 * span
    fa = frame_start(live, rows, span)
    fa_prev = frame_start(live_prev, rows, span)
    a_frame = lax.dynamic_slice_in_dim(masked, fa, a_len, 0)
    b_frame = masked[:b_len]
    from_below = shifted(a_frame, "sector", 1)
    from_above = shifted(b_frame, "sector", -1)
    j = jnp.arange(a_len)
    i0 = j + fa - live + m0h
    i1 = j + fa - live + m0h + m1h
    v0 = (i0 >= 0) & (i0 < m0h)
    v1 = (i1 >= 0) & (i1 < m1h)
    p0 = shift_rows(from_above, fa - live + m0h, a_len)
    p1 = shift_rows(from_above, fa - live + 2 * m0h + m1h, a_len)
    ang = take_angles(angles[0][sector_id], i0, v0) + take_angles(angles[1][sector_id], i1, v1)
    partner = jnp.where(v0[:, None, None], p0, p1).astype(jnp.float32)
    own = a_frame.astype(jnp.float32)
    c = jnp.cos(ang)[:, None, None]
    s = jnp.sin(ang)[:, None, None]
    new_a = jnp.where((v0 | v1)[:, None, None], c * own - s * partner, own).astype(jnp.bfloat16)
    jb = jnp.arange(b_len)
    k0 = jb
    k1 = jb - m0p
    w0 = k0 < m0p
    w1 = (k1 >= 0) & (k1 < m1p)
    q0 = shift_rows(from_below, live_prev - m0p - fa_prev, b_len)
    q1 = shift_rows(from_below, live_prev - 2 * m0p - m1p - fa_prev, b_len)
    angb = take_angles(angles[0][prev_id], k0, w0) + take_angles(angles[1][prev_id], k1, w1)
    partner_b = jnp.where(w0[:, None, None], q0, q1).astype(jnp.float32)
    ownb = b_frame.astype(jnp.float32)
    cb = jnp.cos(angb)[:, None, None]
    sb = jnp.sin(angb)[:, None, None]
    new_b = jnp.where((w0 | w1)[:, None, None], sb * partner_b + cb * ownb, ownb).astype(jnp.bfloat16)
    return masked, new_a, fa, new_b


def dot(a, b):
    return jnp.dot(a, b, precision=HI, preferred_element_type=jnp.float32)


def factor_inverse_kernel(d_ref, o_ref):
    n = d_ref.shape[0]
    a = d_ref[...]
    eye_rows = lax.broadcasted_iota(jnp.int32, (n, n), 0)
    w = (eye_rows == lax.broadcasted_iota(jnp.int32, (n, n), 1)).astype(jnp.float32)
    for first in range(0, n, PHASE):
        m = n - first
        lane = lax.broadcasted_iota(jnp.int32, (m, n), 1)
        sub = lax.broadcasted_iota(jnp.int32, (m, n), 0)
        lane_row = lax.broadcasted_iota(jnp.int32, (1, n), 1)
        sub_col = lax.broadcasted_iota(jnp.int32, (m, 1), 0)

        def body(t, carry, first=first, lane=lane, sub=sub, lane_row=lane_row, sub_col=sub_col):
            a, w = carry
            j = first + t
            col = jnp.sum(jnp.where(lane == j, a, 0.0), axis=1, keepdims=True)
            row = jnp.sum(jnp.where(sub == t, a, 0.0), axis=0, keepdims=True)
            piv = jnp.sum(jnp.where(lane_row == j, row, 0.0), axis=1, keepdims=True)
            r = lax.rsqrt(piv)
            lcol = jnp.where(sub_col >= t, col * r, 0.0)
            lrow = jnp.where(lane_row >= j, row * r, 0.0)
            a = a - lcol * lrow
            wj = jnp.sum(jnp.where(sub == t, w, 0.0), axis=0, keepdims=True) * r
            w = jnp.where(sub == t, wj, w - lcol * wj)
            return a, w

        a, w = lax.fori_loop(0, PHASE, body, (a, w), unroll=PHASE)
        o_ref[first:first + PHASE, :] = w[:PHASE]
        a = a[PHASE:]
        w = w[PHASE:]


def factor_inverse(diag):
    n = diag.shape[0]
    return pl.pallas_call(
        factor_inverse_kernel,
        out_shape=jax.ShapeDtypeStruct((n, n), jnp.float32),
        cost_estimate=pl.CostEstimate(
            flops=6 * n * n * n, transcendentals=n, bytes_accessed=8 * n * n
        ),
    )(diag)


def cholesky_solve(gram, rhs):
    n = gram.shape[0]
    trailing = gram
    rest = rhs
    solved = []
    for start in range(0, n, BLOCK):
        diag = trailing[:BLOCK, :BLOCK]
        inverse = factor_inverse(diag)
        head = dot(inverse, rest[:BLOCK])
        solved.append(head)
        if start + BLOCK < n:
            panel = lax.dot_general(
                trailing[BLOCK:, :BLOCK], inverse, (((1,), (1,)), ((), ())),
                precision=HI, preferred_element_type=jnp.float32,
            )
            trailing = trailing[BLOCK:, BLOCK:] - lax.dot_general(
                panel, panel, (((1,), (1,)), ((), ())),
                precision=HI, preferred_element_type=jnp.float32,
            )
            rest = rest[BLOCK:] - dot(panel, head)
    return jnp.concatenate(solved, 0)


def per_device(amplitudes, next_site, sector_rows, moves, angles, ranks):
    sector_id = lax.axis_index("sector")
    rows = amplitudes.shape[0]
    row_index = jnp.arange(rows)
    live_rows = sector_rows[sector_id]
    masked, new_a, a_start, new_b = build_block(amplitudes, sector_rows, moves, angles)
    site_tensor = next_site[0]
    partial = jnp.einsum("prk,lpr->kl", site_tensor, masked, preferred_element_type=jnp.float32)
    partial_a = jnp.einsum("prk,lpr->kl", site_tensor, new_a, preferred_element_type=jnp.float32)
    partial_b = jnp.einsum("prk,lpr->kl", site_tensor, new_b, preferred_element_type=jnp.float32)
    partial = lax.dynamic_update_slice_in_dim(partial, partial_a, a_start, 1)
    partial = lax.dynamic_update_slice_in_dim(partial, partial_b, 0, 1)
    contracted = lax.psum_scatter(
        partial,
        "row",
        scatter_dimension=0,
        tiled=True,
    ).astype(jnp.bfloat16)
    gathered = lax.all_gather(contracted, "row", axis=0, tiled=True)
    gram_matrix = lax.dot_general(
        gathered, gathered, (((0,), (0,)), ((), ())), preferred_element_type=jnp.float32
    )
    dead_rows = (row_index >= live_rows).astype(jnp.float32)
    gram_matrix = gram_matrix + jnp.diag(dead_rows)
    solved = cholesky_solve(gram_matrix, contracted.astype(jnp.float32).T).T
    kept_mask = ((row_index >= live_rows - ranks[sector_id]) & (row_index < live_rows)).astype(
        jnp.float32
    )
    return (solved * math.sqrt(KOUT) * kept_mask[None, :]).astype(jnp.bfloat16)


def solution(mesh):
    placed = (P("sector", None, "row"), P("sector", None, "row", None), P(), P(), P(), P())
    return jax.shard_map(
        per_device, mesh=mesh, in_specs=placed, out_specs=P("row", "sector"), check_vma=False
    )
```

```python
import math

import jax
import jax.numpy as jnp
from jax import lax
from jax.experimental import pallas as pl
from jax.sharding import PartitionSpec as P

KOUT = 2048
BLOCK = 128
PHASE = 16
UNROLL = 4
HI = lax.Precision.HIGHEST


def shifted(x, axis, by):
    size = lax.axis_size(axis)
    pairs = [(i, i + by) for i in range(size) if 0 <= i + by < size]
    return lax.ppermute(x, axis, pairs)


def rotated_window(own, partner, angle, count, sign):
    slot_index = jnp.arange(own.shape[0])
    own32 = own.astype(jnp.float32)
    partner32 = partner.astype(jnp.float32)
    cos_t = jnp.cos(angle)[:, None, None]
    sin_t = jnp.sin(angle)[:, None, None]
    if sign < 0:
        new = cos_t * own32 - sin_t * partner32
    else:
        new = sin_t * partner32 + cos_t * own32
    return jnp.where((slot_index < count)[:, None, None], new, own32).astype(jnp.bfloat16)


def dot(a, b):
    return jnp.dot(a, b, precision=HI, preferred_element_type=jnp.float32)


def factor_inverse_kernel(d_ref, o_ref):
    n = d_ref.shape[0]
    a = d_ref[...]
    rows_n = lax.broadcasted_iota(jnp.int32, (n, n), 0)
    lanes_n = lax.broadcasted_iota(jnp.int32, (n, n), 1)
    w = (rows_n == lanes_n).astype(jnp.float32)
    diag = jnp.sum(jnp.where(rows_n == lanes_n, a, 0.0), axis=0, keepdims=True)
    for first in range(0, n, PHASE):
        m = n - first
        lane = lax.broadcasted_iota(jnp.int32, (m, n), 1)
        sub = lax.broadcasted_iota(jnp.int32, (m, n), 0)
        lane_row = lax.broadcasted_iota(jnp.int32, (1, n), 1)
        sub_col = lax.broadcasted_iota(jnp.int32, (m, 1), 0)

        def body(t, carry, first=first, lane=lane, sub=sub, lane_row=lane_row, sub_col=sub_col):
            a, w, diag = carry
            j = first + t
            col = jnp.sum(jnp.where(lane == j, a, 0.0), axis=1, keepdims=True)
            row = jnp.sum(jnp.where(sub == t, a, 0.0), axis=0, keepdims=True)
            piv = jnp.sum(jnp.where(lane_row == j, diag, 0.0), axis=1, keepdims=True)
            r = lax.rsqrt(piv)
            lcol = jnp.where(sub_col >= t, col * r, 0.0)
            lrow = jnp.where(lane_row >= j, row * r, 0.0)
            a = a - lcol * lrow
            diag = diag - lrow * lrow
            wj = jnp.sum(jnp.where(sub == t, w, 0.0), axis=0, keepdims=True) * r
            w = jnp.where(sub == t, wj, w - lcol * wj)
            return a, w, diag

        a, w, diag = lax.fori_loop(0, PHASE, body, (a, w, diag), unroll=UNROLL)
        o_ref[first:first + PHASE, :] = w[:PHASE]
        a = a[PHASE:]
        w = w[PHASE:]


def factor_inverse(diag):
    n = diag.shape[0]
    return pl.pallas_call(
        factor_inverse_kernel,
        out_shape=jax.ShapeDtypeStruct((n, n), jnp.float32),
        cost_estimate=pl.CostEstimate(
            flops=6 * n * n * n, transcendentals=n, bytes_accessed=8 * n * n
        ),
    )(diag)


def cholesky_solve(gram, rhs):
    n = gram.shape[0]
    trailing = gram
    rest = rhs
    solved = []
    for start in range(0, n, BLOCK):
        diag = trailing[:BLOCK, :BLOCK]
        inverse = factor_inverse(diag)
        head = dot(inverse, rest[:BLOCK])
        solved.append(head)
        if start + BLOCK < n:
            panel = lax.dot_general(
                trailing[BLOCK:, :BLOCK], inverse, (((1,), (1,)), ((), ())),
                precision=HI, preferred_element_type=jnp.float32,
            )
            trailing = trailing[BLOCK:, BLOCK:] - lax.dot_general(
                panel, panel, (((1,), (1,)), ((), ())),
                precision=HI, preferred_element_type=jnp.float32,
            )
            rest = rest[BLOCK:] - dot(panel, head)
    return jnp.concatenate(solved, 0)


def per_device(amplitudes, next_site, sector_rows, moves, angles, ranks):
    sector_id = lax.axis_index("sector")
    rows = amplitudes.shape[0]
    move_rows = angles.shape[-1]
    row_index = jnp.arange(rows)
    live_rows = sector_rows[sector_id]
    prev_id = jnp.maximum(sector_id - 1, 0)
    count_here = moves[:, sector_id]
    count_prev = jnp.where(sector_id > 0, moves[:, prev_id], 0)
    masked = jnp.where((row_index < live_rows)[:, None, None], amplitudes, jnp.zeros((), amplitudes.dtype))
    padded = jnp.concatenate(
        [masked, jnp.zeros((move_rows,) + masked.shape[1:], masked.dtype)], 0
    )
    starts_a = [live_rows - count_here[0], live_rows - count_here[0] - count_here[1]]
    starts_b = [jnp.int32(0), count_prev[0]]
    own_a = [lax.dynamic_slice_in_dim(padded, s, move_rows, 0) for s in starts_a]
    own_b = [lax.dynamic_slice_in_dim(padded, s, move_rows, 0) for s in starts_b]
    from_below = [shifted(w, "sector", 1) for w in own_a]
    from_above = [shifted(w, "sector", -1) for w in own_b]
    new_a = [
        rotated_window(own_a[g], from_above[g], angles[g][sector_id], count_here[g], -1)
        for g in range(2)
    ]
    new_b = [
        rotated_window(own_b[g], from_below[g], angles[g][prev_id], count_prev[g], 1)
        for g in range(2)
    ]
    padded = lax.dynamic_update_slice_in_dim(padded, new_a[1], starts_a[1], 0)
    padded = lax.dynamic_update_slice_in_dim(padded, new_a[0], starts_a[0], 0)
    padded = lax.dynamic_update_slice_in_dim(padded, new_b[0], starts_b[0], 0)
    padded = lax.dynamic_update_slice_in_dim(padded, new_b[1], starts_b[1], 0)
    block_rows = padded[:rows]
    site_tensor = next_site[0]
    contracted = lax.psum_scatter(
        jnp.einsum("prk,lpr->kl", site_tensor, block_rows, preferred_element_type=jnp.float32),
        "row",
        scatter_dimension=0,
        tiled=True,
    ).astype(jnp.bfloat16)
    gathered = lax.all_gather(contracted, "row", axis=0, tiled=True)
    gram_matrix = lax.dot_general(
        gathered, gathered, (((0,), (0,)), ((), ())), preferred_element_type=jnp.float32
    )
    dead_rows = (row_index >= live_rows).astype(jnp.float32)
    gram_matrix = gram_matrix + jnp.diag(dead_rows)
    solved = cholesky_solve(gram_matrix, contracted.astype(jnp.float32).T).T
    kept_mask = ((row_index >= live_rows - ranks[sector_id]) & (row_index < live_rows)).astype(
        jnp.float32
    )
    return (solved * math.sqrt(KOUT) * kept_mask[None, :]).astype(jnp.bfloat16)


def solution(mesh):
    placed = (P("sector", None, "row"), P("sector", None, "row", None), P(), P(), P(), P())
    return jax.shard_map(
        per_device, mesh=mesh, in_specs=placed, out_specs=P("row", "sector"), check_vma=False
    )
```

```python
import math

import jax
import jax.numpy as jnp
from jax import lax
from jax.experimental import pallas as pl
from jax.sharding import PartitionSpec as P

KOUT = 2048
BLOCK = 128
CHUNK = 256
PHASE = 16
UNROLL = 4
HI = lax.Precision.HIGHEST


def shifted(x, axis, by):
    size = lax.axis_size(axis)
    pairs = [(i, i + by) for i in range(size) if 0 <= i + by < size]
    return lax.ppermute(x, axis, pairs)


def rotated_window(own, partner, angle, count, sign):
    slot_index = jnp.arange(own.shape[0])
    own32 = own.astype(jnp.float32)
    partner32 = partner.astype(jnp.float32)
    cos_t = jnp.cos(angle)[:, None, None]
    sin_t = jnp.sin(angle)[:, None, None]
    if sign < 0:
        new = cos_t * own32 - sin_t * partner32
    else:
        new = sin_t * partner32 + cos_t * own32
    return jnp.where((slot_index < count)[:, None, None], new, own32).astype(jnp.bfloat16)


def dot(a, b):
    return jnp.dot(a, b, precision=HI, preferred_element_type=jnp.float32)


def factor_inverse_kernel(d_ref, o_ref):
    n = d_ref.shape[0]
    a = d_ref[...]
    rows_n = lax.broadcasted_iota(jnp.int32, (n, n), 0)
    lanes_n = lax.broadcasted_iota(jnp.int32, (n, n), 1)
    w = (rows_n == lanes_n).astype(jnp.float32)
    diag = jnp.sum(jnp.where(rows_n == lanes_n, a, 0.0), axis=0, keepdims=True)
    for first in range(0, n, PHASE):
        m = n - first
        lane = lax.broadcasted_iota(jnp.int32, (m, n), 1)
        sub = lax.broadcasted_iota(jnp.int32, (m, n), 0)
        lane_row = lax.broadcasted_iota(jnp.int32, (1, n), 1)
        sub_col = lax.broadcasted_iota(jnp.int32, (m, 1), 0)

        def body(t, carry, first=first, lane=lane, sub=sub, lane_row=lane_row, sub_col=sub_col):
            a, w, diag = carry
            j = first + t
            col = jnp.sum(jnp.where(lane == j, a, 0.0), axis=1, keepdims=True)
            row = jnp.sum(jnp.where(sub == t, a, 0.0), axis=0, keepdims=True)
            piv = jnp.sum(jnp.where(lane_row == j, diag, 0.0), axis=1, keepdims=True)
            r = lax.rsqrt(piv)
            lcol = jnp.where(sub_col >= t, col * r, 0.0)
            lrow = jnp.where(lane_row >= j, row * r, 0.0)
            a = a - lcol * lrow
            diag = diag - lrow * lrow
            wj = jnp.sum(jnp.where(sub == t, w, 0.0), axis=0, keepdims=True) * r
            w = jnp.where(sub == t, wj, w - lcol * wj)
            return a, w, diag

        a, w, diag = lax.fori_loop(0, PHASE, body, (a, w, diag), unroll=UNROLL)
        o_ref[first:first + PHASE, :] = w[:PHASE]
        a = a[PHASE:]
        w = w[PHASE:]


def factor_inverse(diag):
    n = diag.shape[0]
    return pl.pallas_call(
        factor_inverse_kernel,
        out_shape=jax.ShapeDtypeStruct((n, n), jnp.float32),
        cost_estimate=pl.CostEstimate(
            flops=6 * n * n * n, transcendentals=n, bytes_accessed=8 * n * n
        ),
    )(diag)


def bordered_solve(chunks, rhs_blocks, dead_blocks):
    lead_inverse = None
    solved = None
    for k, cols in enumerate(chunks):
        seen = jnp.concatenate(chunks[: k + 1], 1) if k else cols
        gram_row = lax.dot_general(
            cols, seen, (((0,), (0,)), ((), ())), preferred_element_type=jnp.float32
        )
        diag = gram_row[:, k * BLOCK:] + jnp.diag(dead_blocks[k])
        rhs = rhs_blocks[k]
        if k:
            row = lax.dot_general(
                gram_row[:, : k * BLOCK], lead_inverse, (((1,), (1,)), ((), ())),
                precision=HI, preferred_element_type=jnp.float32,
            )
            diag = diag - lax.dot_general(
                row, row, (((1,), (1,)), ((), ())),
                precision=HI, preferred_element_type=jnp.float32,
            )
            rhs = rhs - dot(row, solved)
        inverse = factor_inverse(diag)
        head = dot(inverse, rhs)
        if k == 0:
            lead_inverse = inverse
            solved = head
        else:
            below = -dot(inverse, dot(row, lead_inverse))
            width = lead_inverse.shape[0]
            lead_inverse = jnp.concatenate(
                [
                    jnp.concatenate([lead_inverse, jnp.zeros((width, BLOCK), jnp.float32)], 1),
                    jnp.concatenate([below, inverse], 1),
                ],
                0,
            )
            solved = jnp.concatenate([solved, head], 0)
    return solved


def per_device(amplitudes, next_site, sector_rows, moves, angles, ranks):
    sector_id = lax.axis_index("sector")
    rows = amplitudes.shape[0]
    move_rows = angles.shape[-1]
    row_index = jnp.arange(rows)
    live_rows = sector_rows[sector_id]
    prev_id = jnp.maximum(sector_id - 1, 0)
    count_here = moves[:, sector_id]
    count_prev = jnp.where(sector_id > 0, moves[:, prev_id], 0)
    masked = jnp.where((row_index < live_rows)[:, None, None], amplitudes, jnp.zeros((), amplitudes.dtype))
    padded = jnp.concatenate(
        [masked, jnp.zeros((move_rows,) + masked.shape[1:], masked.dtype)], 0
    )
    starts_a = [live_rows - count_here[0], live_rows - count_here[0] - count_here[1]]
    starts_b = [jnp.int32(0), count_prev[0]]
    own_a = [lax.dynamic_slice_in_dim(padded, s, move_rows, 0) for s in starts_a]
    own_b = [lax.dynamic_slice_in_dim(padded, s, move_rows, 0) for s in starts_b]
    from_below = [shifted(w, "sector", 1) for w in own_a]
    from_above = [shifted(w, "sector", -1) for w in own_b]
    new_a = [
        rotated_window(own_a[g], from_above[g], angles[g][sector_id], count_here[g], -1)
        for g in range(2)
    ]
    new_b = [
        rotated_window(own_b[g], from_below[g], angles[g][prev_id], count_prev[g], 1)
        for g in range(2)
    ]
    padded = lax.dynamic_update_slice_in_dim(padded, new_a[1], starts_a[1], 0)
    padded = lax.dynamic_update_slice_in_dim(padded, new_a[0], starts_a[0], 0)
    padded = lax.dynamic_update_slice_in_dim(padded, new_b[0], starts_b[0], 0)
    padded = lax.dynamic_update_slice_in_dim(padded, new_b[1], starts_b[1], 0)
    block_rows = padded[:rows]
    site_tensor = next_site[0]
    partial = jnp.einsum("prk,lpr->kl", site_tensor, block_rows, preferred_element_type=jnp.float32)
    dead_rows = (row_index >= live_rows).astype(jnp.float32)
    chunks, rhs_blocks, dead_blocks = [], [], []
    for start in range(0, rows, CHUNK):
        local = lax.psum_scatter(
            partial[:, start:start + CHUNK], "row", scatter_dimension=0, tiled=True
        ).astype(jnp.bfloat16)
        gathered = lax.all_gather(local, "row", axis=0, tiled=True)
        for sub in range(0, CHUNK, BLOCK):
            chunks.append(gathered[:, sub:sub + BLOCK])
            rhs_blocks.append(local[:, sub:sub + BLOCK].astype(jnp.float32).T)
            dead_blocks.append(dead_rows[start + sub:start + sub + BLOCK])
    solved = bordered_solve(chunks, rhs_blocks, dead_blocks).T
    kept_mask = ((row_index >= live_rows - ranks[sector_id]) & (row_index < live_rows)).astype(
        jnp.float32
    )
    return (solved * math.sqrt(KOUT) * kept_mask[None, :]).astype(jnp.bfloat16)


def solution(mesh):
    placed = (P("sector", None, "row"), P("sector", None, "row", None), P(), P(), P(), P())
    return jax.shard_map(
        per_device, mesh=mesh, in_specs=placed, out_specs=P("row", "sector"), check_vma=False
    )
```

```python
import math

import jax
import jax.numpy as jnp
from jax import lax
from jax.experimental import pallas as pl
from jax.experimental.pallas import tpu as pltpu
from jax.sharding import PartitionSpec as P

KOUT = 2048
BLOCK = 128
PHASE = 16
UNROLL = 4
HI = lax.Precision.HIGHEST


def shifted(x, axis, by):
    size = lax.axis_size(axis)
    pairs = [(i, i + by) for i in range(size) if 0 <= i + by < size]
    return lax.ppermute(x, axis, pairs)


def rotated_window(own, partner, angle, count, sign):
    slot_index = jnp.arange(own.shape[0])
    own32 = own.astype(jnp.float32)
    partner32 = partner.astype(jnp.float32)
    cos_t = jnp.cos(angle)[:, None, None]
    sin_t = jnp.sin(angle)[:, None, None]
    if sign < 0:
        new = cos_t * own32 - sin_t * partner32
    else:
        new = sin_t * partner32 + cos_t * own32
    return jnp.where((slot_index < count)[:, None, None], new, own32).astype(jnp.bfloat16)


def dot(a, b):
    return jnp.dot(a, b, precision=HI, preferred_element_type=jnp.float32)


def block_inverse(a):
    n = a.shape[0]
    rows_n = lax.broadcasted_iota(jnp.int32, (n, n), 0)
    lanes_n = lax.broadcasted_iota(jnp.int32, (n, n), 1)
    w = (rows_n == lanes_n).astype(jnp.float32)
    diag = jnp.sum(jnp.where(rows_n == lanes_n, a, 0.0), axis=0, keepdims=True)
    done = []
    for first in range(0, n, PHASE):
        m = n - first
        lane = lax.broadcasted_iota(jnp.int32, (m, n), 1)
        sub = lax.broadcasted_iota(jnp.int32, (m, n), 0)
        lane_row = lax.broadcasted_iota(jnp.int32, (1, n), 1)
        sub_col = lax.broadcasted_iota(jnp.int32, (m, 1), 0)

        def body(t, carry, first=first, lane=lane, sub=sub, lane_row=lane_row, sub_col=sub_col):
            a, w, diag = carry
            j = first + t
            col = jnp.sum(jnp.where(lane == j, a, 0.0), axis=1, keepdims=True)
            row = jnp.sum(jnp.where(sub == t, a, 0.0), axis=0, keepdims=True)
            piv = jnp.sum(jnp.where(lane_row == j, diag, 0.0), axis=1, keepdims=True)
            r = lax.rsqrt(piv)
            lcol = jnp.where(sub_col >= t, col * r, 0.0)
            lrow = jnp.where(lane_row >= j, row * r, 0.0)
            a = a - lcol * lrow
            diag = diag - lrow * lrow
            wj = jnp.sum(jnp.where(sub == t, w, 0.0), axis=0, keepdims=True) * r
            w = jnp.where(sub == t, wj, w - lcol * wj)
            return a, w, diag

        a, w, diag = lax.fori_loop(0, PHASE, body, (a, w, diag), unroll=UNROLL)
        done.append(w[:PHASE])
        a = a[PHASE:]
        w = w[PHASE:]
    return jnp.concatenate(done, 0)


def mm(a, b, transpose_b=False):
    dims = (((1,), (1 if transpose_b else 0,)), ((), ()))
    return lax.dot_general(a, b, dims, precision=HI, preferred_element_type=jnp.float32)


def solve_kernel(g_ref, b_ref, x_ref, t_ref, r_ref):
    n = g_ref.shape[0]
    t_ref[...] = g_ref[...]
    r_ref[...] = b_ref[...]
    for start in range(0, n, BLOCK):
        end = start + BLOCK
        inverse = block_inverse(t_ref[start:end, start:end])
        head = mm(inverse, r_ref[start:end, :])
        x_ref[start:end, :] = head
        if end < n:
            panel = mm(t_ref[end:, start:end], inverse, transpose_b=True)
            t_ref[end:, end:] = t_ref[end:, end:] - mm(panel, panel, transpose_b=True)
            r_ref[end:, :] = r_ref[end:, :] - mm(panel, head)


def cholesky_solve(gram, rhs):
    n, m = rhs.shape
    return pl.pallas_call(
        solve_kernel,
        out_shape=jax.ShapeDtypeStruct((n, m), jnp.float32),
        scratch_shapes=[pltpu.VMEM((n, n), jnp.float32), pltpu.VMEM((n, m), jnp.float32)],
        compiler_params=pltpu.CompilerParams(vmem_limit_bytes=48 * 1024 * 1024),
    )(gram, rhs)


def per_device(amplitudes, next_site, sector_rows, moves, angles, ranks):
    sector_id = lax.axis_index("sector")
    rows = amplitudes.shape[0]
    move_rows = angles.shape[-1]
    row_index = jnp.arange(rows)
    live_rows = sector_rows[sector_id]
    prev_id = jnp.maximum(sector_id - 1, 0)
    count_here = moves[:, sector_id]
    count_prev = jnp.where(sector_id > 0, moves[:, prev_id], 0)
    masked = jnp.where((row_index < live_rows)[:, None, None], amplitudes, jnp.zeros((), amplitudes.dtype))
    padded = jnp.concatenate(
        [masked, jnp.zeros((move_rows,) + masked.shape[1:], masked.dtype)], 0
    )
    starts_a = [live_rows - count_here[0], live_rows - count_here[0] - count_here[1]]
    starts_b = [jnp.int32(0), count_prev[0]]
    own_a = [lax.dynamic_slice_in_dim(padded, s, move_rows, 0) for s in starts_a]
    own_b = [lax.dynamic_slice_in_dim(padded, s, move_rows, 0) for s in starts_b]
    from_below = [shifted(w, "sector", 1) for w in own_a]
    from_above = [shifted(w, "sector", -1) for w in own_b]
    new_a = [
        rotated_window(own_a[g], from_above[g], angles[g][sector_id], count_here[g], -1)
        for g in range(2)
    ]
    new_b = [
        rotated_window(own_b[g], from_below[g], angles[g][prev_id], count_prev[g], 1)
        for g in range(2)
    ]
    padded = lax.dynamic_update_slice_in_dim(padded, new_a[1], starts_a[1], 0)
    padded = lax.dynamic_update_slice_in_dim(padded, new_a[0], starts_a[0], 0)
    padded = lax.dynamic_update_slice_in_dim(padded, new_b[0], starts_b[0], 0)
    padded = lax.dynamic_update_slice_in_dim(padded, new_b[1], starts_b[1], 0)
    block_rows = padded[:rows]
    site_tensor = next_site[0]
    contracted = lax.psum_scatter(
        jnp.einsum("prk,lpr->kl", site_tensor, block_rows, preferred_element_type=jnp.float32),
        "row",
        scatter_dimension=0,
        tiled=True,
    ).astype(jnp.bfloat16)
    gathered = lax.all_gather(contracted, "row", axis=0, tiled=True)
    gram_matrix = lax.dot_general(
        gathered, gathered, (((0,), (0,)), ((), ())), preferred_element_type=jnp.float32
    )
    dead_rows = (row_index >= live_rows).astype(jnp.float32)
    gram_matrix = gram_matrix + jnp.diag(dead_rows)
    solved = cholesky_solve(gram_matrix, contracted.astype(jnp.float32).T).T
    kept_mask = ((row_index >= live_rows - ranks[sector_id]) & (row_index < live_rows)).astype(
        jnp.float32
    )
    return (solved * math.sqrt(KOUT) * kept_mask[None, :]).astype(jnp.bfloat16)


def solution(mesh):
    placed = (P("sector", None, "row"), P("sector", None, "row", None), P(), P(), P(), P())
    return jax.shard_map(
        per_device, mesh=mesh, in_specs=placed, out_specs=P("row", "sector"), check_vma=False
    )
```

```python
import math

import jax
import jax.numpy as jnp
from jax import lax
from jax.experimental import pallas as pl
from jax.experimental.pallas import tpu as pltpu
from jax.sharding import PartitionSpec as P

KOUT = 2048
BLOCK = 128
PHASE = 16
UNROLL = 4
HI = lax.Precision.HIGHEST


def shifted(x, axis, by):
    size = lax.axis_size(axis)
    pairs = [(i, i + by) for i in range(size) if 0 <= i + by < size]
    return lax.ppermute(x, axis, pairs)


def rotated_window(own, partner, angle, count, sign):
    slot_index = jnp.arange(own.shape[0])
    own32 = own.astype(jnp.float32)
    partner32 = partner.astype(jnp.float32)
    cos_t = jnp.cos(angle)[:, None, None]
    sin_t = jnp.sin(angle)[:, None, None]
    if sign < 0:
        new = cos_t * own32 - sin_t * partner32
    else:
        new = sin_t * partner32 + cos_t * own32
    return jnp.where((slot_index < count)[:, None, None], new, own32).astype(jnp.bfloat16)


def dot(a, b):
    return jnp.dot(a, b, precision=HI, preferred_element_type=jnp.float32)


def block_inverse(a):
    n = a.shape[0]
    rows_n = lax.broadcasted_iota(jnp.int32, (n, n), 0)
    lanes_n = lax.broadcasted_iota(jnp.int32, (n, n), 1)
    w = (rows_n == lanes_n).astype(jnp.float32)
    diag = jnp.sum(jnp.where(rows_n == lanes_n, a, 0.0), axis=0, keepdims=True)
    done = []
    for first in range(0, n, PHASE):
        m = n - first
        lane = lax.broadcasted_iota(jnp.int32, (m, n), 1)
        sub = lax.broadcasted_iota(jnp.int32, (m, n), 0)
        lane_row = lax.broadcasted_iota(jnp.int32, (1, n), 1)
        sub_col = lax.broadcasted_iota(jnp.int32, (m, 1), 0)

        def body(t, carry, first=first, lane=lane, sub=sub, lane_row=lane_row, sub_col=sub_col):
            a, w, diag = carry
            j = first + t
            col = jnp.sum(jnp.where(lane == j, a, 0.0), axis=1, keepdims=True)
            row = jnp.sum(jnp.where(sub == t, a, 0.0), axis=0, keepdims=True)
            piv = jnp.sum(jnp.where(lane_row == j, diag, 0.0), axis=1, keepdims=True)
            r = lax.rsqrt(piv)
            lcol = jnp.where(sub_col >= t, col * r, 0.0)
            lrow = jnp.where(lane_row >= j, row * r, 0.0)
            a = a - lcol * lrow
            diag = diag - lrow * lrow
            wj = jnp.sum(jnp.where(sub == t, w, 0.0), axis=0, keepdims=True) * r
            w = jnp.where(sub == t, wj, w - lcol * wj)
            return a, w, diag

        a, w, diag = lax.fori_loop(0, PHASE, body, (a, w, diag), unroll=UNROLL)
        done.append(w[:PHASE])
        a = a[PHASE:]
        w = w[PHASE:]
    return jnp.concatenate(done, 0)


def mm(a, b, transpose_b=False):
    dims = (((1,), (1 if transpose_b else 0,)), ((), ()))
    return lax.dot_general(a, b, dims, precision=HI, preferred_element_type=jnp.float32)


def solve_kernel(g_ref, b_ref, x_ref, t_ref, r_ref):
    n = g_ref.shape[0]
    t_ref[...] = g_ref[...]
    r_ref[...] = b_ref[...]
    for start in range(0, n, BLOCK):
        end = start + BLOCK
        inverse = block_inverse(t_ref[start:end, start:end])
        head = mm(inverse, r_ref[start:end, :])
        x_ref[start:end, :] = head
        if end < n:
            panel = mm(t_ref[end:, start:end], inverse, transpose_b=True)
            t_ref[end:, end:] = t_ref[end:, end:] - mm(panel, panel, transpose_b=True)
            r_ref[end:, :] = r_ref[end:, :] - mm(panel, head)


def cholesky_solve(gram, rhs):
    n, m = rhs.shape
    return pl.pallas_call(
        solve_kernel,
        out_shape=jax.ShapeDtypeStruct((n, m), jnp.float32),
        scratch_shapes=[pltpu.VMEM((n, n), jnp.float32), pltpu.VMEM((n, m), jnp.float32)],
        compiler_params=pltpu.CompilerParams(vmem_limit_bytes=48 * 1024 * 1024),
    )(gram, rhs)


def per_device(amplitudes, next_site, sector_rows, moves, angles, ranks):
    sector_id = lax.axis_index("sector")
    rows = amplitudes.shape[0]
    move_rows = angles.shape[-1]
    row_index = jnp.arange(rows)
    live_rows = sector_rows[sector_id]
    prev_id = jnp.maximum(sector_id - 1, 0)
    count_here = moves[:, sector_id]
    count_prev = jnp.where(sector_id > 0, moves[:, prev_id], 0)
    masked = jnp.where((row_index < live_rows)[:, None, None], amplitudes, jnp.zeros((), amplitudes.dtype))
    padded = jnp.concatenate(
        [masked, jnp.zeros((move_rows,) + masked.shape[1:], masked.dtype)], 0
    )
    starts_a = [live_rows - count_here[0], live_rows - count_here[0] - count_here[1]]
    starts_b = [jnp.int32(0), count_prev[0]]
    own_a = [lax.dynamic_slice_in_dim(padded, s, move_rows, 0) for s in starts_a]
    own_b = [lax.dynamic_slice_in_dim(padded, s, move_rows, 0) for s in starts_b]
    from_below = shifted(jnp.stack(own_a), "sector", 1)
    from_above = shifted(jnp.stack(own_b), "sector", -1)
    new_a = [
        rotated_window(own_a[g], from_above[g], angles[g][sector_id], count_here[g], -1)
        for g in range(2)
    ]
    new_b = [
        rotated_window(own_b[g], from_below[g], angles[g][prev_id], count_prev[g], 1)
        for g in range(2)
    ]
    padded = lax.dynamic_update_slice_in_dim(padded, new_a[1], starts_a[1], 0)
    padded = lax.dynamic_update_slice_in_dim(padded, new_a[0], starts_a[0], 0)
    padded = lax.dynamic_update_slice_in_dim(padded, new_b[0], starts_b[0], 0)
    padded = lax.dynamic_update_slice_in_dim(padded, new_b[1], starts_b[1], 0)
    block_rows = padded[:rows]
    site_tensor = next_site[0]
    contracted = lax.psum_scatter(
        jnp.einsum("prk,lpr->kl", site_tensor, block_rows, preferred_element_type=jnp.float32),
        "row",
        scatter_dimension=0,
        tiled=True,
    ).astype(jnp.bfloat16)
    gathered = lax.all_gather(contracted, "row", axis=0, tiled=True)
    gram_matrix = lax.dot_general(
        gathered, gathered, (((0,), (0,)), ((), ())), preferred_element_type=jnp.float32
    )
    dead_rows = (row_index >= live_rows).astype(jnp.float32)
    gram_matrix = gram_matrix + jnp.diag(dead_rows)
    solved = cholesky_solve(gram_matrix, contracted.astype(jnp.float32).T).T
    kept_mask = ((row_index >= live_rows - ranks[sector_id]) & (row_index < live_rows)).astype(
        jnp.float32
    )
    return (solved * math.sqrt(KOUT) * kept_mask[None, :]).astype(jnp.bfloat16)


def solution(mesh):
    placed = (P("sector", None, "row"), P("sector", None, "row", None), P(), P(), P(), P())
    return jax.shard_map(
        per_device, mesh=mesh, in_specs=placed, out_specs=P("row", "sector"), check_vma=False
    )
```

```python
import math

import jax
import jax.numpy as jnp
from jax import lax
from jax.experimental import pallas as pl
from jax.experimental.pallas import tpu as pltpu
from jax.sharding import PartitionSpec as P

KOUT = 2048
BLOCK = 128
PHASE = 16
UNROLL = 4
HI = lax.Precision.HIGHEST


def shifted(x, axis, by):
    size = lax.axis_size(axis)
    pairs = [(i, i + by) for i in range(size) if 0 <= i + by < size]
    return lax.ppermute(x, axis, pairs)


def rotated_window(own, partner, angle, count, sign):
    slot_index = jnp.arange(own.shape[0])
    own32 = own.astype(jnp.float32)
    partner32 = partner.astype(jnp.float32)
    cos_t = jnp.cos(angle)[:, None, None]
    sin_t = jnp.sin(angle)[:, None, None]
    if sign < 0:
        new = cos_t * own32 - sin_t * partner32
    else:
        new = sin_t * partner32 + cos_t * own32
    return jnp.where((slot_index < count)[:, None, None], new, own32).astype(jnp.bfloat16)


def dot(a, b):
    return jnp.dot(a, b, precision=HI, preferred_element_type=jnp.float32)


def block_inverse(a):
    n = a.shape[0]
    rows_n = lax.broadcasted_iota(jnp.int32, (n, n), 0)
    lanes_n = lax.broadcasted_iota(jnp.int32, (n, n), 1)
    w = (rows_n == lanes_n).astype(jnp.float32)
    diag = jnp.sum(jnp.where(rows_n == lanes_n, a, 0.0), axis=0, keepdims=True)
    done = []
    for first in range(0, n, PHASE):
        m = n - first
        lane = lax.broadcasted_iota(jnp.int32, (m, n), 1)
        sub = lax.broadcasted_iota(jnp.int32, (m, n), 0)
        lane_row = lax.broadcasted_iota(jnp.int32, (1, n), 1)
        sub_col = lax.broadcasted_iota(jnp.int32, (m, 1), 0)

        def body(s, carry, first=first, lane=lane, sub=sub, lane_row=lane_row, sub_col=sub_col):
            a, w, diag = carry
            t = 2 * s
            j = first + t
            col0 = jnp.sum(jnp.where(lane == j, a, 0.0), axis=1, keepdims=True)
            col1 = jnp.sum(jnp.where(lane == j + 1, a, 0.0), axis=1, keepdims=True)
            row0 = jnp.sum(jnp.where(sub == t, a, 0.0), axis=0, keepdims=True)
            row1 = jnp.sum(jnp.where(sub == t + 1, a, 0.0), axis=0, keepdims=True)
            d0 = jnp.sum(jnp.where(lane_row == j, diag, 0.0), axis=1, keepdims=True)
            d1 = jnp.sum(jnp.where(lane_row == j + 1, diag, 0.0), axis=1, keepdims=True)
            off = jnp.sum(jnp.where(lane_row == j, row1, 0.0), axis=1, keepdims=True)
            r0 = lax.rsqrt(d0)
            l10 = off * r0
            r1 = lax.rsqrt(d1 - l10 * l10)
            lcol0 = jnp.where(sub_col >= t, col0 * r0, 0.0)
            lrow0 = jnp.where(lane_row >= j, row0 * r0, 0.0)
            lcol1 = jnp.where(sub_col >= t + 1, (col1 - lcol0 * l10) * r1, 0.0)
            lrow1 = jnp.where(lane_row >= j + 1, (row1 - lrow0 * l10) * r1, 0.0)
            a = a - lcol0 * lrow0 - lcol1 * lrow1
            diag = diag - lrow0 * lrow0 - lrow1 * lrow1
            w0 = jnp.sum(jnp.where(sub == t, w, 0.0), axis=0, keepdims=True) * r0
            w1 = (jnp.sum(jnp.where(sub == t + 1, w, 0.0), axis=0, keepdims=True) - l10 * w0) * r1
            w = jnp.where(
                sub == t, w0, jnp.where(sub == t + 1, w1, w - lcol0 * w0 - lcol1 * w1)
            )
            return a, w, diag

        a, w, diag = lax.fori_loop(0, PHASE // 2, body, (a, w, diag), unroll=UNROLL)
        done.append(w[:PHASE])
        a = a[PHASE:]
        w = w[PHASE:]
    return jnp.concatenate(done, 0)


def mm(a, b, transpose_b=False):
    dims = (((1,), (1 if transpose_b else 0,)), ((), ()))
    return lax.dot_general(a, b, dims, precision=HI, preferred_element_type=jnp.float32)


def solve_kernel(g_ref, b_ref, x_ref, t_ref, r_ref):
    n = g_ref.shape[0]
    t_ref[...] = g_ref[...]
    r_ref[...] = b_ref[...]
    for start in range(0, n, BLOCK):
        end = start + BLOCK
        inverse = block_inverse(t_ref[start:end, start:end])
        head = mm(inverse, r_ref[start:end, :])
        x_ref[start:end, :] = head
        if end < n:
            panel = mm(t_ref[end:, start:end], inverse, transpose_b=True)
            t_ref[end:, end:] = t_ref[end:, end:] - mm(panel, panel, transpose_b=True)
            r_ref[end:, :] = r_ref[end:, :] - mm(panel, head)


def cholesky_solve(gram, rhs):
    n, m = rhs.shape
    return pl.pallas_call(
        solve_kernel,
        out_shape=jax.ShapeDtypeStruct((n, m), jnp.float32),
        scratch_shapes=[pltpu.VMEM((n, n), jnp.float32), pltpu.VMEM((n, m), jnp.float32)],
        compiler_params=pltpu.CompilerParams(vmem_limit_bytes=48 * 1024 * 1024),
    )(gram, rhs)


def per_device(amplitudes, next_site, sector_rows, moves, angles, ranks):
    sector_id = lax.axis_index("sector")
    rows = amplitudes.shape[0]
    move_rows = angles.shape[-1]
    row_index = jnp.arange(rows)
    live_rows = sector_rows[sector_id]
    prev_id = jnp.maximum(sector_id - 1, 0)
    count_here = moves[:, sector_id]
    count_prev = jnp.where(sector_id > 0, moves[:, prev_id], 0)
    masked = jnp.where((row_index < live_rows)[:, None, None], amplitudes, jnp.zeros((), amplitudes.dtype))
    padded = jnp.concatenate(
        [masked, jnp.zeros((move_rows,) + masked.shape[1:], masked.dtype)], 0
    )
    starts_a = [live_rows - count_here[0], live_rows - count_here[0] - count_here[1]]
    starts_b = [jnp.int32(0), count_prev[0]]
    own_a = [lax.dynamic_slice_in_dim(padded, s, move_rows, 0) for s in starts_a]
    own_b = [lax.dynamic_slice_in_dim(padded, s, move_rows, 0) for s in starts_b]
    from_below = shifted(jnp.stack(own_a), "sector", 1)
    from_above = shifted(jnp.stack(own_b), "sector", -1)
    new_a = [
        rotated_window(own_a[g], from_above[g], angles[g][sector_id], count_here[g], -1)
        for g in range(2)
    ]
    new_b = [
        rotated_window(own_b[g], from_below[g], angles[g][prev_id], count_prev[g], 1)
        for g in range(2)
    ]
    padded = lax.dynamic_update_slice_in_dim(padded, new_a[1], starts_a[1], 0)
    padded = lax.dynamic_update_slice_in_dim(padded, new_a[0], starts_a[0], 0)
    padded = lax.dynamic_update_slice_in_dim(padded, new_b[0], starts_b[0], 0)
    padded = lax.dynamic_update_slice_in_dim(padded, new_b[1], starts_b[1], 0)
    block_rows = padded[:rows]
    site_tensor = next_site[0]
    contracted = lax.psum_scatter(
        jnp.einsum("prk,lpr->kl", site_tensor, block_rows, preferred_element_type=jnp.float32),
        "row",
        scatter_dimension=0,
        tiled=True,
    ).astype(jnp.bfloat16)
    gathered = lax.all_gather(contracted, "row", axis=0, tiled=True)
    gram_matrix = lax.dot_general(
        gathered, gathered, (((0,), (0,)), ((), ())), preferred_element_type=jnp.float32
    )
    dead_rows = (row_index >= live_rows).astype(jnp.float32)
    gram_matrix = gram_matrix + jnp.diag(dead_rows)
    solved = cholesky_solve(gram_matrix, contracted.astype(jnp.float32).T).T
    kept_mask = ((row_index >= live_rows - ranks[sector_id]) & (row_index < live_rows)).astype(
        jnp.float32
    )
    return (solved * math.sqrt(KOUT) * kept_mask[None, :]).astype(jnp.bfloat16)


def solution(mesh):
    placed = (P("sector", None, "row"), P("sector", None, "row", None), P(), P(), P(), P())
    return jax.shard_map(
        per_device, mesh=mesh, in_specs=placed, out_specs=P("row", "sector"), check_vma=False
    )
```

```python
import math

import jax
import jax.numpy as jnp
from jax import lax
from jax.experimental import pallas as pl
from jax.experimental.pallas import tpu as pltpu
from jax.sharding import PartitionSpec as P

KOUT = 2048
BLOCK = 128
PHASE = 16
UNROLL = 4
STEP = 4
HI = lax.Precision.HIGHEST


def shifted(x, axis, by):
    size = lax.axis_size(axis)
    pairs = [(i, i + by) for i in range(size) if 0 <= i + by < size]
    return lax.ppermute(x, axis, pairs)


def rotated_window(own, partner, angle, count, sign):
    slot_index = jnp.arange(own.shape[0])
    own32 = own.astype(jnp.float32)
    partner32 = partner.astype(jnp.float32)
    cos_t = jnp.cos(angle)[:, None, None]
    sin_t = jnp.sin(angle)[:, None, None]
    if sign < 0:
        new = cos_t * own32 - sin_t * partner32
    else:
        new = sin_t * partner32 + cos_t * own32
    return jnp.where((slot_index < count)[:, None, None], new, own32).astype(jnp.bfloat16)


def dot(a, b):
    return jnp.dot(a, b, precision=HI, preferred_element_type=jnp.float32)


def block_inverse(a):
    n = a.shape[0]
    rows_n = lax.broadcasted_iota(jnp.int32, (n, n), 0)
    lanes_n = lax.broadcasted_iota(jnp.int32, (n, n), 1)
    w = (rows_n == lanes_n).astype(jnp.float32)
    diag = jnp.sum(jnp.where(rows_n == lanes_n, a, 0.0), axis=0, keepdims=True)
    done = []
    for first in range(0, n, PHASE):
        m = n - first
        lane = lax.broadcasted_iota(jnp.int32, (m, n), 1)
        sub = lax.broadcasted_iota(jnp.int32, (m, n), 0)
        lane_row = lax.broadcasted_iota(jnp.int32, (1, n), 1)
        sub_col = lax.broadcasted_iota(jnp.int32, (m, 1), 0)

        def body(s, carry, first=first, lane=lane, sub=sub, lane_row=lane_row, sub_col=sub_col):
            a, w, diag = carry
            t = STEP * s
            j = first + t
            cols = [jnp.sum(jnp.where(lane == j + q, a, 0.0), axis=1, keepdims=True) for q in range(STEP)]
            rows = [jnp.sum(jnp.where(sub == t + q, a, 0.0), axis=0, keepdims=True) for q in range(STEP)]
            pivots = [jnp.sum(jnp.where(lane_row == j + q, diag, 0.0), axis=1, keepdims=True) for q in range(STEP)]
            low = [[jnp.sum(jnp.where(lane_row == j + p, rows[q], 0.0), axis=1, keepdims=True) for p in range(q)] for q in range(STEP)]
            inv = []
            for q in range(STEP):
                for p in range(q):
                    value = low[q][p]
                    for u in range(p):
                        value = value - low[q][u] * low[p][u]
                    low[q][p] = value * inv[p]
                piv = pivots[q]
                for u in range(q):
                    piv = piv - low[q][u] * low[q][u]
                inv.append(lax.rsqrt(piv))
            lcols, lrows, wrows = [], [], []
            for q in range(STEP):
                col, row = cols[q], rows[q]
                wrow = jnp.sum(jnp.where(sub == t + q, w, 0.0), axis=0, keepdims=True)
                for p in range(q):
                    col = col - lcols[p] * low[q][p]
                    row = row - lrows[p] * low[q][p]
                    wrow = wrow - low[q][p] * wrows[p]
                lcols.append(jnp.where(sub_col >= t + q, col * inv[q], 0.0))
                lrows.append(jnp.where(lane_row >= j + q, row * inv[q], 0.0))
                wrows.append(wrow * inv[q])
            rest = w
            for q in range(STEP):
                a = a - lcols[q] * lrows[q]
                diag = diag - lrows[q] * lrows[q]
                rest = rest - lcols[q] * wrows[q]
            for q in reversed(range(STEP)):
                rest = jnp.where(sub == t + q, wrows[q], rest)
            return a, rest, diag

        a, w, diag = lax.fori_loop(0, PHASE // STEP, body, (a, w, diag), unroll=UNROLL)
        done.append(w[:PHASE])
        a = a[PHASE:]
        w = w[PHASE:]
    return jnp.concatenate(done, 0)


def mm(a, b, transpose_b=False):
    dims = (((1,), (1 if transpose_b else 0,)), ((), ()))
    return lax.dot_general(a, b, dims, precision=HI, preferred_element_type=jnp.float32)


def solve_kernel(g_ref, b_ref, x_ref, t_ref, r_ref):
    n = g_ref.shape[0]
    t_ref[...] = g_ref[...]
    r_ref[...] = b_ref[...]
    for start in range(0, n, BLOCK):
        end = start + BLOCK
        inverse = block_inverse(t_ref[start:end, start:end])
        head = mm(inverse, r_ref[start:end, :])
        x_ref[start:end, :] = head
        if end < n:
            panel = mm(t_ref[end:, start:end], inverse, transpose_b=True)
            t_ref[end:, end:] = t_ref[end:, end:] - mm(panel, panel, transpose_b=True)
            r_ref[end:, :] = r_ref[end:, :] - mm(panel, head)


def cholesky_solve(gram, rhs):
    n, m = rhs.shape
    return pl.pallas_call(
        solve_kernel,
        out_shape=jax.ShapeDtypeStruct((n, m), jnp.float32),
        scratch_shapes=[pltpu.VMEM((n, n), jnp.float32), pltpu.VMEM((n, m), jnp.float32)],
        compiler_params=pltpu.CompilerParams(vmem_limit_bytes=48 * 1024 * 1024),
    )(gram, rhs)


def per_device(amplitudes, next_site, sector_rows, moves, angles, ranks):
    sector_id = lax.axis_index("sector")
    rows = amplitudes.shape[0]
    move_rows = angles.shape[-1]
    row_index = jnp.arange(rows)
    live_rows = sector_rows[sector_id]
    prev_id = jnp.maximum(sector_id - 1, 0)
    count_here = moves[:, sector_id]
    count_prev = jnp.where(sector_id > 0, moves[:, prev_id], 0)
    masked = jnp.where((row_index < live_rows)[:, None, None], amplitudes, jnp.zeros((), amplitudes.dtype))
    padded = jnp.concatenate(
        [masked, jnp.zeros((move_rows,) + masked.shape[1:], masked.dtype)], 0
    )
    starts_a = [live_rows - count_here[0], live_rows - count_here[0] - count_here[1]]
    starts_b = [jnp.int32(0), count_prev[0]]
    own_a = [lax.dynamic_slice_in_dim(padded, s, move_rows, 0) for s in starts_a]
    own_b = [lax.dynamic_slice_in_dim(padded, s, move_rows, 0) for s in starts_b]
    from_below = shifted(jnp.stack(own_a), "sector", 1)
    from_above = shifted(jnp.stack(own_b), "sector", -1)
    new_a = [
        rotated_window(own_a[g], from_above[g], angles[g][sector_id], count_here[g], -1)
        for g in range(2)
    ]
    new_b = [
        rotated_window(own_b[g], from_below[g], angles[g][prev_id], count_prev[g], 1)
        for g in range(2)
    ]
    padded = lax.dynamic_update_slice_in_dim(padded, new_a[1], starts_a[1], 0)
    padded = lax.dynamic_update_slice_in_dim(padded, new_a[0], starts_a[0], 0)
    padded = lax.dynamic_update_slice_in_dim(padded, new_b[0], starts_b[0], 0)
    padded = lax.dynamic_update_slice_in_dim(padded, new_b[1], starts_b[1], 0)
    block_rows = padded[:rows]
    site_tensor = next_site[0]
    contracted = lax.psum_scatter(
        jnp.einsum("prk,lpr->kl", site_tensor, block_rows, preferred_element_type=jnp.float32),
        "row",
        scatter_dimension=0,
        tiled=True,
    ).astype(jnp.bfloat16)
    gathered = lax.all_gather(contracted, "row", axis=0, tiled=True)
    gram_matrix = lax.dot_general(
        gathered, gathered, (((0,), (0,)), ((), ())), preferred_element_type=jnp.float32
    )
    dead_rows = (row_index >= live_rows).astype(jnp.float32)
    gram_matrix = gram_matrix + jnp.diag(dead_rows)
    solved = cholesky_solve(gram_matrix, contracted.astype(jnp.float32).T).T
    kept_mask = ((row_index >= live_rows - ranks[sector_id]) & (row_index < live_rows)).astype(
        jnp.float32
    )
    return (solved * math.sqrt(KOUT) * kept_mask[None, :]).astype(jnp.bfloat16)


def solution(mesh):
    placed = (P("sector", None, "row"), P("sector", None, "row", None), P(), P(), P(), P())
    return jax.shard_map(
        per_device, mesh=mesh, in_specs=placed, out_specs=P("row", "sector"), check_vma=False
    )
```

```python
import math

import jax
import jax.numpy as jnp
from jax import lax
from jax.experimental import pallas as pl
from jax.experimental.pallas import tpu as pltpu
from jax.sharding import PartitionSpec as P

KOUT = 2048
BLOCK = 128
PHASE = 16
UNROLL = 4
STEP = 8
HI = lax.Precision.HIGHEST


def shifted(x, axis, by):
    size = lax.axis_size(axis)
    pairs = [(i, i + by) for i in range(size) if 0 <= i + by < size]
    return lax.ppermute(x, axis, pairs)


def rotated_window(own, partner, angle, count, sign):
    slot_index = jnp.arange(own.shape[0])
    own32 = own.astype(jnp.float32)
    partner32 = partner.astype(jnp.float32)
    cos_t = jnp.cos(angle)[:, None, None]
    sin_t = jnp.sin(angle)[:, None, None]
    if sign < 0:
        new = cos_t * own32 - sin_t * partner32
    else:
        new = sin_t * partner32 + cos_t * own32
    return jnp.where((slot_index < count)[:, None, None], new, own32).astype(jnp.bfloat16)


def dot(a, b):
    return jnp.dot(a, b, precision=HI, preferred_element_type=jnp.float32)


def block_inverse(a):
    n = a.shape[0]
    rows_n = lax.broadcasted_iota(jnp.int32, (n, n), 0)
    lanes_n = lax.broadcasted_iota(jnp.int32, (n, n), 1)
    w = (rows_n == lanes_n).astype(jnp.float32)
    diag = jnp.sum(jnp.where(rows_n == lanes_n, a, 0.0), axis=0, keepdims=True)
    done = []
    for first in range(0, n, PHASE):
        m = n - first
        lane = lax.broadcasted_iota(jnp.int32, (m, n), 1)
        sub = lax.broadcasted_iota(jnp.int32, (m, n), 0)
        lane_row = lax.broadcasted_iota(jnp.int32, (1, n), 1)
        sub_col = lax.broadcasted_iota(jnp.int32, (m, 1), 0)

        def body(s, carry, first=first, lane=lane, sub=sub, lane_row=lane_row, sub_col=sub_col):
            a, w, diag = carry
            t = STEP * s
            j = first + t
            cols = [jnp.sum(jnp.where(lane == j + q, a, 0.0), axis=1, keepdims=True) for q in range(STEP)]
            rows = [jnp.sum(jnp.where(sub == t + q, a, 0.0), axis=0, keepdims=True) for q in range(STEP)]
            pivots = [jnp.sum(jnp.where(lane_row == j + q, diag, 0.0), axis=1, keepdims=True) for q in range(STEP)]
            low = [[jnp.sum(jnp.where(lane_row == j + p, rows[q], 0.0), axis=1, keepdims=True) for p in range(q)] for q in range(STEP)]
            inv = []
            for q in range(STEP):
                for p in range(q):
                    value = low[q][p]
                    for u in range(p):
                        value = value - low[q][u] * low[p][u]
                    low[q][p] = value * inv[p]
                piv = pivots[q]
                for u in range(q):
                    piv = piv - low[q][u] * low[q][u]
                inv.append(lax.rsqrt(piv))
            lcols, lrows, wrows = [], [], []
            for q in range(STEP):
                col, row = cols[q], rows[q]
                wrow = jnp.sum(jnp.where(sub == t + q, w, 0.0), axis=0, keepdims=True)
                for p in range(q):
                    col = col - lcols[p] * low[q][p]
                    row = row - lrows[p] * low[q][p]
                    wrow = wrow - low[q][p] * wrows[p]
                lcols.append(jnp.where(sub_col >= t + q, col * inv[q], 0.0))
                lrows.append(jnp.where(lane_row >= j + q, row * inv[q], 0.0))
                wrows.append(wrow * inv[q])
            rest = w
            for q in range(STEP):
                a = a - lcols[q] * lrows[q]
                diag = diag - lrows[q] * lrows[q]
                rest = rest - lcols[q] * wrows[q]
            for q in reversed(range(STEP)):
                rest = jnp.where(sub == t + q, wrows[q], rest)
            return a, rest, diag

        a, w, diag = lax.fori_loop(0, PHASE // STEP, body, (a, w, diag), unroll=UNROLL)
        done.append(w[:PHASE])
        a = a[PHASE:]
        w = w[PHASE:]
    return jnp.concatenate(done, 0)


def mm(a, b, transpose_b=False):
    dims = (((1,), (1 if transpose_b else 0,)), ((), ()))
    return lax.dot_general(a, b, dims, precision=HI, preferred_element_type=jnp.float32)


def solve_kernel(g_ref, b_ref, x_ref, t_ref, r_ref):
    n = g_ref.shape[0]
    t_ref[...] = g_ref[...]
    r_ref[...] = b_ref[...]
    for start in range(0, n, BLOCK):
        end = start + BLOCK
        inverse = block_inverse(t_ref[start:end, start:end])
        head = mm(inverse, r_ref[start:end, :])
        x_ref[start:end, :] = head
        if end < n:
            panel = mm(t_ref[end:, start:end], inverse, transpose_b=True)
            t_ref[end:, end:] = t_ref[end:, end:] - mm(panel, panel, transpose_b=True)
            r_ref[end:, :] = r_ref[end:, :] - mm(panel, head)


def cholesky_solve(gram, rhs):
    n, m = rhs.shape
    return pl.pallas_call(
        solve_kernel,
        out_shape=jax.ShapeDtypeStruct((n, m), jnp.float32),
        scratch_shapes=[pltpu.VMEM((n, n), jnp.float32), pltpu.VMEM((n, m), jnp.float32)],
        compiler_params=pltpu.CompilerParams(vmem_limit_bytes=48 * 1024 * 1024),
    )(gram, rhs)


def per_device(amplitudes, next_site, sector_rows, moves, angles, ranks):
    sector_id = lax.axis_index("sector")
    rows = amplitudes.shape[0]
    move_rows = angles.shape[-1]
    row_index = jnp.arange(rows)
    live_rows = sector_rows[sector_id]
    prev_id = jnp.maximum(sector_id - 1, 0)
    count_here = moves[:, sector_id]
    count_prev = jnp.where(sector_id > 0, moves[:, prev_id], 0)
    masked = jnp.where((row_index < live_rows)[:, None, None], amplitudes, jnp.zeros((), amplitudes.dtype))
    padded = jnp.concatenate(
        [masked, jnp.zeros((move_rows,) + masked.shape[1:], masked.dtype)], 0
    )
    starts_a = [live_rows - count_here[0], live_rows - count_here[0] - count_here[1]]
    starts_b = [jnp.int32(0), count_prev[0]]
    own_a = [lax.dynamic_slice_in_dim(padded, s, move_rows, 0) for s in starts_a]
    own_b = [lax.dynamic_slice_in_dim(padded, s, move_rows, 0) for s in starts_b]
    from_below = shifted(jnp.stack(own_a), "sector", 1)
    from_above = shifted(jnp.stack(own_b), "sector", -1)
    new_a = [
        rotated_window(own_a[g], from_above[g], angles[g][sector_id], count_here[g], -1)
        for g in range(2)
    ]
    new_b = [
        rotated_window(own_b[g], from_below[g], angles[g][prev_id], count_prev[g], 1)
        for g in range(2)
    ]
    padded = lax.dynamic_update_slice_in_dim(padded, new_a[1], starts_a[1], 0)
    padded = lax.dynamic_update_slice_in_dim(padded, new_a[0], starts_a[0], 0)
    padded = lax.dynamic_update_slice_in_dim(padded, new_b[0], starts_b[0], 0)
    padded = lax.dynamic_update_slice_in_dim(padded, new_b[1], starts_b[1], 0)
    block_rows = padded[:rows]
    site_tensor = next_site[0]
    contracted = lax.psum_scatter(
        jnp.einsum("prk,lpr->kl", site_tensor, block_rows, preferred_element_type=jnp.float32),
        "row",
        scatter_dimension=0,
        tiled=True,
    ).astype(jnp.bfloat16)
    gathered = lax.all_gather(contracted, "row", axis=0, tiled=True)
    gram_matrix = lax.dot_general(
        gathered, gathered, (((0,), (0,)), ((), ())), preferred_element_type=jnp.float32
    )
    dead_rows = (row_index >= live_rows).astype(jnp.float32)
    gram_matrix = gram_matrix + jnp.diag(dead_rows)
    solved = cholesky_solve(gram_matrix, contracted.astype(jnp.float32).T).T
    kept_mask = ((row_index >= live_rows - ranks[sector_id]) & (row_index < live_rows)).astype(
        jnp.float32
    )
    return (solved * math.sqrt(KOUT) * kept_mask[None, :]).astype(jnp.bfloat16)


def solution(mesh):
    placed = (P("sector", None, "row"), P("sector", None, "row", None), P(), P(), P(), P())
    return jax.shard_map(
        per_device, mesh=mesh, in_specs=placed, out_specs=P("row", "sector"), check_vma=False
    )
```

```python
import math

import jax
import jax.numpy as jnp
from jax import lax
from jax.experimental import pallas as pl
from jax.experimental.pallas import tpu as pltpu
from jax.sharding import PartitionSpec as P

KOUT = 2048
BLOCK = 128
PHASE = 16
UNROLL = 1
STEP = 4
HI = lax.Precision.HIGHEST


def shifted(x, axis, by):
    size = lax.axis_size(axis)
    pairs = [(i, i + by) for i in range(size) if 0 <= i + by < size]
    return lax.ppermute(x, axis, pairs)


def rotated_window(own, partner, angle, count, sign):
    slot_index = jnp.arange(own.shape[0])
    own32 = own.astype(jnp.float32)
    partner32 = partner.astype(jnp.float32)
    cos_t = jnp.cos(angle)[:, None, None]
    sin_t = jnp.sin(angle)[:, None, None]
    if sign < 0:
        new = cos_t * own32 - sin_t * partner32
    else:
        new = sin_t * partner32 + cos_t * own32
    return jnp.where((slot_index < count)[:, None, None], new, own32).astype(jnp.bfloat16)


def dot(a, b):
    return jnp.dot(a, b, precision=HI, preferred_element_type=jnp.float32)


def block_inverse(a):
    n = a.shape[0]
    rows_n = lax.broadcasted_iota(jnp.int32, (n, n), 0)
    lanes_n = lax.broadcasted_iota(jnp.int32, (n, n), 1)
    w = (rows_n == lanes_n).astype(jnp.float32)
    diag = jnp.sum(jnp.where(rows_n == lanes_n, a, 0.0), axis=0, keepdims=True)
    done = []
    for first in range(0, n, PHASE):
        m = n - first
        lane = lax.broadcasted_iota(jnp.int32, (m, n), 1)
        sub = lax.broadcasted_iota(jnp.int32, (m, n), 0)
        lane_row = lax.broadcasted_iota(jnp.int32, (1, n), 1)
        sub_col = lax.broadcasted_iota(jnp.int32, (m, 1), 0)

        def body(s, carry, first=first, lane=lane, sub=sub, lane_row=lane_row, sub_col=sub_col):
            a, w, diag = carry
            t = STEP * s
            j = first + t
            cols = [jnp.sum(jnp.where(lane == j + q, a, 0.0), axis=1, keepdims=True) for q in range(STEP)]
            rows = [jnp.sum(jnp.where(sub == t + q, a, 0.0), axis=0, keepdims=True) for q in range(STEP)]
            pivots = [jnp.sum(jnp.where(lane_row == j + q, diag, 0.0), axis=1, keepdims=True) for q in range(STEP)]
            low = [[jnp.sum(jnp.where(lane_row == j + p, rows[q], 0.0), axis=1, keepdims=True) for p in range(q)] for q in range(STEP)]
            inv = []
            for q in range(STEP):
                for p in range(q):
                    value = low[q][p]
                    for u in range(p):
                        value = value - low[q][u] * low[p][u]
                    low[q][p] = value * inv[p]
                piv = pivots[q]
                for u in range(q):
                    piv = piv - low[q][u] * low[q][u]
                inv.append(lax.rsqrt(piv))
            lcols, lrows, wrows = [], [], []
            for q in range(STEP):
                col, row = cols[q], rows[q]
                wrow = jnp.sum(jnp.where(sub == t + q, w, 0.0), axis=0, keepdims=True)
                for p in range(q):
                    col = col - lcols[p] * low[q][p]
                    row = row - lrows[p] * low[q][p]
                    wrow = wrow - low[q][p] * wrows[p]
                lcols.append(jnp.where(sub_col >= t + q, col * inv[q], 0.0))
                lrows.append(jnp.where(lane_row >= j + q, row * inv[q], 0.0))
                wrows.append(wrow * inv[q])
            rest = w
            for q in range(STEP):
                a = a - lcols[q] * lrows[q]
                diag = diag - lrows[q] * lrows[q]
                rest = rest - lcols[q] * wrows[q]
            for q in reversed(range(STEP)):
                rest = jnp.where(sub == t + q, wrows[q], rest)
            return a, rest, diag

        a, w, diag = lax.fori_loop(0, PHASE // STEP, body, (a, w, diag), unroll=UNROLL)
        done.append(w[:PHASE])
        a = a[PHASE:]
        w = w[PHASE:]
    return jnp.concatenate(done, 0)


def mm(a, b, transpose_b=False):
    dims = (((1,), (1 if transpose_b else 0,)), ((), ()))
    return lax.dot_general(a, b, dims, precision=HI, preferred_element_type=jnp.float32)


def solve_kernel(g_ref, b_ref, x_ref, t_ref, r_ref):
    n = g_ref.shape[0]
    t_ref[...] = g_ref[...]
    r_ref[...] = b_ref[...]
    for start in range(0, n, BLOCK):
        end = start + BLOCK
        inverse = block_inverse(t_ref[start:end, start:end])
        head = mm(inverse, r_ref[start:end, :])
        x_ref[start:end, :] = head
        if end < n:
            panel = mm(t_ref[end:, start:end], inverse, transpose_b=True)
            t_ref[end:, end:] = t_ref[end:, end:] - mm(panel, panel, transpose_b=True)
            r_ref[end:, :] = r_ref[end:, :] - mm(panel, head)


def cholesky_solve(gram, rhs):
    n, m = rhs.shape
    return pl.pallas_call(
        solve_kernel,
        out_shape=jax.ShapeDtypeStruct((n, m), jnp.float32),
        scratch_shapes=[pltpu.VMEM((n, n), jnp.float32), pltpu.VMEM((n, m), jnp.float32)],
        compiler_params=pltpu.CompilerParams(vmem_limit_bytes=48 * 1024 * 1024),
    )(gram, rhs)


def per_device(amplitudes, next_site, sector_rows, moves, angles, ranks):
    sector_id = lax.axis_index("sector")
    rows = amplitudes.shape[0]
    move_rows = angles.shape[-1]
    row_index = jnp.arange(rows)
    live_rows = sector_rows[sector_id]
    prev_id = jnp.maximum(sector_id - 1, 0)
    count_here = moves[:, sector_id]
    count_prev = jnp.where(sector_id > 0, moves[:, prev_id], 0)
    masked = jnp.where((row_index < live_rows)[:, None, None], amplitudes, jnp.zeros((), amplitudes.dtype))
    padded = jnp.concatenate(
        [masked, jnp.zeros((move_rows,) + masked.shape[1:], masked.dtype)], 0
    )
    starts_a = [live_rows - count_here[0], live_rows - count_here[0] - count_here[1]]
    starts_b = [jnp.int32(0), count_prev[0]]
    own_a = [lax.dynamic_slice_in_dim(padded, s, move_rows, 0) for s in starts_a]
    own_b = [lax.dynamic_slice_in_dim(padded, s, move_rows, 0) for s in starts_b]
    from_below = shifted(jnp.stack(own_a), "sector", 1)
    from_above = shifted(jnp.stack(own_b), "sector", -1)
    new_a = [
        rotated_window(own_a[g], from_above[g], angles[g][sector_id], count_here[g], -1)
        for g in range(2)
    ]
    new_b = [
        rotated_window(own_b[g], from_below[g], angles[g][prev_id], count_prev[g], 1)
        for g in range(2)
    ]
    padded = lax.dynamic_update_slice_in_dim(padded, new_a[1], starts_a[1], 0)
    padded = lax.dynamic_update_slice_in_dim(padded, new_a[0], starts_a[0], 0)
    padded = lax.dynamic_update_slice_in_dim(padded, new_b[0], starts_b[0], 0)
    padded = lax.dynamic_update_slice_in_dim(padded, new_b[1], starts_b[1], 0)
    block_rows = padded[:rows]
    site_tensor = next_site[0]
    contracted = lax.psum_scatter(
        jnp.einsum("prk,lpr->kl", site_tensor, block_rows, preferred_element_type=jnp.float32),
        "row",
        scatter_dimension=0,
        tiled=True,
    ).astype(jnp.bfloat16)
    gathered = lax.all_gather(contracted, "row", axis=0, tiled=True)
    gram_matrix = lax.dot_general(
        gathered, gathered, (((0,), (0,)), ((), ())), preferred_element_type=jnp.float32
    )
    dead_rows = (row_index >= live_rows).astype(jnp.float32)
    gram_matrix = gram_matrix + jnp.diag(dead_rows)
    solved = cholesky_solve(gram_matrix, contracted.astype(jnp.float32).T).T
    kept_mask = ((row_index >= live_rows - ranks[sector_id]) & (row_index < live_rows)).astype(
        jnp.float32
    )
    return (solved * math.sqrt(KOUT) * kept_mask[None, :]).astype(jnp.bfloat16)


def solution(mesh):
    placed = (P("sector", None, "row"), P("sector", None, "row", None), P(), P(), P(), P())
    return jax.shard_map(
        per_device, mesh=mesh, in_specs=placed, out_specs=P("row", "sector"), check_vma=False
    )
```

```python
import math

import jax
import jax.numpy as jnp
from jax import lax
from jax.experimental import pallas as pl
from jax.experimental.pallas import tpu as pltpu
from jax.sharding import PartitionSpec as P

KOUT = 2048
BLOCK = 128
PHASE = 8
UNROLL = 2
STEP = 4
HI = lax.Precision.HIGHEST


def shifted(x, axis, by):
    size = lax.axis_size(axis)
    pairs = [(i, i + by) for i in range(size) if 0 <= i + by < size]
    return lax.ppermute(x, axis, pairs)


def rotated_window(own, partner, angle, count, sign):
    slot_index = jnp.arange(own.shape[0])
    own32 = own.astype(jnp.float32)
    partner32 = partner.astype(jnp.float32)
    cos_t = jnp.cos(angle)[:, None, None]
    sin_t = jnp.sin(angle)[:, None, None]
    if sign < 0:
        new = cos_t * own32 - sin_t * partner32
    else:
        new = sin_t * partner32 + cos_t * own32
    return jnp.where((slot_index < count)[:, None, None], new, own32).astype(jnp.bfloat16)


def dot(a, b):
    return jnp.dot(a, b, precision=HI, preferred_element_type=jnp.float32)


def block_inverse(a):
    n = a.shape[0]
    rows_n = lax.broadcasted_iota(jnp.int32, (n, n), 0)
    lanes_n = lax.broadcasted_iota(jnp.int32, (n, n), 1)
    w = (rows_n == lanes_n).astype(jnp.float32)
    diag = jnp.sum(jnp.where(rows_n == lanes_n, a, 0.0), axis=0, keepdims=True)
    done = []
    for first in range(0, n, PHASE):
        m = n - first
        lane = lax.broadcasted_iota(jnp.int32, (m, n), 1)
        sub = lax.broadcasted_iota(jnp.int32, (m, n), 0)
        lane_row = lax.broadcasted_iota(jnp.int32, (1, n), 1)
        sub_col = lax.broadcasted_iota(jnp.int32, (m, 1), 0)

        def body(s, carry, first=first, lane=lane, sub=sub, lane_row=lane_row, sub_col=sub_col):
            a, w, diag = carry
            t = STEP * s
            j = first + t
            cols = [jnp.sum(jnp.where(lane == j + q, a, 0.0), axis=1, keepdims=True) for q in range(STEP)]
            rows = [jnp.sum(jnp.where(sub == t + q, a, 0.0), axis=0, keepdims=True) for q in range(STEP)]
            pivots = [jnp.sum(jnp.where(lane_row == j + q, diag, 0.0), axis=1, keepdims=True) for q in range(STEP)]
            low = [[jnp.sum(jnp.where(lane_row == j + p, rows[q], 0.0), axis=1, keepdims=True) for p in range(q)] for q in range(STEP)]
            inv = []
            for q in range(STEP):
                for p in range(q):
                    value = low[q][p]
                    for u in range(p):
                        value = value - low[q][u] * low[p][u]
                    low[q][p] = value * inv[p]
                piv = pivots[q]
                for u in range(q):
                    piv = piv - low[q][u] * low[q][u]
                inv.append(lax.rsqrt(piv))
            lcols, lrows, wrows = [], [], []
            for q in range(STEP):
                col, row = cols[q], rows[q]
                wrow = jnp.sum(jnp.where(sub == t + q, w, 0.0), axis=0, keepdims=True)
                for p in range(q):
                    col = col - lcols[p] * low[q][p]
                    row = row - lrows[p] * low[q][p]
                    wrow = wrow - low[q][p] * wrows[p]
                lcols.append(jnp.where(sub_col >= t + q, col * inv[q], 0.0))
                lrows.append(jnp.where(lane_row >= j + q, row * inv[q], 0.0))
                wrows.append(wrow * inv[q])
            rest = w
            for q in range(STEP):
                a = a - lcols[q] * lrows[q]
                diag = diag - lrows[q] * lrows[q]
                rest = rest - lcols[q] * wrows[q]
            for q in reversed(range(STEP)):
                rest = jnp.where(sub == t + q, wrows[q], rest)
            return a, rest, diag

        a, w, diag = lax.fori_loop(0, PHASE // STEP, body, (a, w, diag), unroll=UNROLL)
        done.append(w[:PHASE])
        a = a[PHASE:]
        w = w[PHASE:]
    return jnp.concatenate(done, 0)


def mm(a, b, transpose_b=False):
    dims = (((1,), (1 if transpose_b else 0,)), ((), ()))
    return lax.dot_general(a, b, dims, precision=HI, preferred_element_type=jnp.float32)


def solve_kernel(g_ref, b_ref, x_ref, t_ref, r_ref):
    n = g_ref.shape[0]
    t_ref[...] = g_ref[...]
    r_ref[...] = b_ref[...]
    for start in range(0, n, BLOCK):
        end = start + BLOCK
        inverse = block_inverse(t_ref[start:end, start:end])
        head = mm(inverse, r_ref[start:end, :])
        x_ref[start:end, :] = head
        if end < n:
            panel = mm(t_ref[end:, start:end], inverse, transpose_b=True)
            t_ref[end:, end:] = t_ref[end:, end:] - mm(panel, panel, transpose_b=True)
            r_ref[end:, :] = r_ref[end:, :] - mm(panel, head)


def cholesky_solve(gram, rhs):
    n, m = rhs.shape
    return pl.pallas_call(
        solve_kernel,
        out_shape=jax.ShapeDtypeStruct((n, m), jnp.float32),
        scratch_shapes=[pltpu.VMEM((n, n), jnp.float32), pltpu.VMEM((n, m), jnp.float32)],
        compiler_params=pltpu.CompilerParams(vmem_limit_bytes=48 * 1024 * 1024),
    )(gram, rhs)


def per_device(amplitudes, next_site, sector_rows, moves, angles, ranks):
    sector_id = lax.axis_index("sector")
    rows = amplitudes.shape[0]
    move_rows = angles.shape[-1]
    row_index = jnp.arange(rows)
    live_rows = sector_rows[sector_id]
    prev_id = jnp.maximum(sector_id - 1, 0)
    count_here = moves[:, sector_id]
    count_prev = jnp.where(sector_id > 0, moves[:, prev_id], 0)
    masked = jnp.where((row_index < live_rows)[:, None, None], amplitudes, jnp.zeros((), amplitudes.dtype))
    padded = jnp.concatenate(
        [masked, jnp.zeros((move_rows,) + masked.shape[1:], masked.dtype)], 0
    )
    starts_a = [live_rows - count_here[0], live_rows - count_here[0] - count_here[1]]
    starts_b = [jnp.int32(0), count_prev[0]]
    own_a = [lax.dynamic_slice_in_dim(padded, s, move_rows, 0) for s in starts_a]
    own_b = [lax.dynamic_slice_in_dim(padded, s, move_rows, 0) for s in starts_b]
    from_below = shifted(jnp.stack(own_a), "sector", 1)
    from_above = shifted(jnp.stack(own_b), "sector", -1)
    new_a = [
        rotated_window(own_a[g], from_above[g], angles[g][sector_id], count_here[g], -1)
        for g in range(2)
    ]
    new_b = [
        rotated_window(own_b[g], from_below[g], angles[g][prev_id], count_prev[g], 1)
        for g in range(2)
    ]
    padded = lax.dynamic_update_slice_in_dim(padded, new_a[1], starts_a[1], 0)
    padded = lax.dynamic_update_slice_in_dim(padded, new_a[0], starts_a[0], 0)
    padded = lax.dynamic_update_slice_in_dim(padded, new_b[0], starts_b[0], 0)
    padded = lax.dynamic_update_slice_in_dim(padded, new_b[1], starts_b[1], 0)
    block_rows = padded[:rows]
    site_tensor = next_site[0]
    contracted = lax.psum_scatter(
        jnp.einsum("prk,lpr->kl", site_tensor, block_rows, preferred_element_type=jnp.float32),
        "row",
        scatter_dimension=0,
        tiled=True,
    ).astype(jnp.bfloat16)
    gathered = lax.all_gather(contracted, "row", axis=0, tiled=True)
    gram_matrix = lax.dot_general(
        gathered, gathered, (((0,), (0,)), ((), ())), preferred_element_type=jnp.float32
    )
    dead_rows = (row_index >= live_rows).astype(jnp.float32)
    gram_matrix = gram_matrix + jnp.diag(dead_rows)
    solved = cholesky_solve(gram_matrix, contracted.astype(jnp.float32).T).T
    kept_mask = ((row_index >= live_rows - ranks[sector_id]) & (row_index < live_rows)).astype(
        jnp.float32
    )
    return (solved * math.sqrt(KOUT) * kept_mask[None, :]).astype(jnp.bfloat16)


def solution(mesh):
    placed = (P("sector", None, "row"), P("sector", None, "row", None), P(), P(), P(), P())
    return jax.shard_map(
        per_device, mesh=mesh, in_specs=placed, out_specs=P("row", "sector"), check_vma=False
    )
```
